512 devices in a mesh: half: 2 (over core), cls: 64 (over z, x), vol: 4 (over y).
Axes of the slice: x: 4, y: 4, z: 16, core: 2. Of those that a mesh axis runs over, the one named last changes fastest.
Arguments:
- images: bfloat16 [16384, 16384], P(('half', 'cls'), 'vol')
- groups: int32 [16384, 1], P(('half', 'cls')), may hold values from 0 to 63; in each aligned block of 128 rows (0 to 127, 128 to 255, ...) at most 4 rows name the same one
- references: bfloat16 [2048, 16384], P('cls', 'vol'), may hold values from -0.046875 to 0.046875
- interp_index: int32 [2048, 16384], P('cls', 'vol'), may hold values from 0 to 2047
- shell_index: int32 [4, 262144], P('vol', ('half', 'cls')), may hold values from 0 to 127
Outputs:
- volume: float32 [4, 262144], P('vol', ('half', 'cls'))
- shell_fsc: float32 [128], replicated
The draws below stay inside these ranges and needn't reach their ends.
Inputs may be any that keep to these rules, and one draw needn't show every extreme that they name: `groups`: within each aligned block of 128 particles no group appears more than 4 times, a bound that some block reaches.
All inputs are finite; a program needn't handle non-finite values.
Results may differ from the reference program's by a relative error of at most 0.00041.
Values may be sent and summed in bfloat16 or wider, within the bound.
No kernel may reach another device: no remote copies, remote signals or barrier semaphores. Data moves between devices by JAX's collectives and lax.ppermute only.
A program may use at most 64 MiB of HBM per device.

```python
import math
import jax
import jax.numpy as jnp
import numpy as np
from jax import lax

IMG = 128
SHIFTS = 5
NSHELL = 128
PART_DEV = 128
CLS_DEV = 32
PLANES = 4
VBOX = 256
PIX = 16384
PIXQ = 4096
VOXS = 262144
CAP = 4
CLASSES = 2048
PARTICLES = 16384
N_HALF = 2
N_CLS = 64
N_VOL = 4


def draw_images(key, part):
    template_key = jax.random.fold_in(key, 11)
    noise_key = jax.random.fold_in(key, 12)
    columns = jnp.arange(IMG, dtype=jnp.float32)
    amplitude = 1.5 * jnp.exp(-4.0 * columns / IMG)
    template = jax.random.normal(template_key, (IMG, IMG), jnp.float32) * amplitude[None, :]
    noise = jax.random.normal(noise_key, (PARTICLES, IMG, IMG), jnp.float32)
    values = template[None, :, :] + noise
    values = jnp.clip(values, -8.0, 8.0)
    return values.reshape(PARTICLES, IMG * IMG).astype(jnp.bfloat16)


def draw_interp_index(key, part):
    band_key = jax.random.fold_in(key, 21)
    depth_key = jax.random.fold_in(key, 22)
    depth = VBOX * PLANES
    band = jax.random.randint(band_key, (CLASSES, IMG * IMG), 0, 2, jnp.int32)
    offset = jax.random.randint(depth_key, (CLASSES, IMG * IMG), 0, depth, jnp.int32)
    return (band * depth + offset).astype(jnp.int32)


def draw_shell_index(key, part):
    jitter_key = jax.random.fold_in(key, 31)
    depth = VBOX * PLANES
    radius = jnp.arange(VOXS, dtype=jnp.int32) // depth
    base = radius * NSHELL // VBOX
    jitter = jax.random.randint(jitter_key, (N_VOL, VOXS), 0, max(NSHELL // 16, 2), jnp.int32)
    return jnp.minimum(base[None, :] + jitter, NSHELL - 1).astype(jnp.int32)


def levels(stream_key, dims, cuts, smallest, high):
    gain, own = 1.0, jax.random.fold_in(stream_key, 6)
    for position, blocks in cuts:
        heights = jnp.exp(jax.random.uniform(jax.random.fold_in(own, position), (blocks,), jnp.float32, smallest / len(cuts), high / len(cuts)))
        gain = gain * jnp.repeat(heights, dims[position] // blocks).reshape([-1 if axis == position else 1 for axis in range(len(dims))])
    return gain


def shared_out(rng, own, number, rows, amount, top, limit, lean):
    sequence = jax.random.permutation(rng, amount)
    heavy_load, ordinary = shares(amount, rows * top, limit, lean, True), shares(amount, rows * top, limit, lean, False)
    places = jnp.arange(amount)

    def named(sizes, offset_by):
        used = int((sizes > 0).sum())
        fixed = max(1, used // 4)
        moved = fixed + (places - fixed + offset_by * (used - fixed)) % max(1, amount - fixed)
        return jnp.zeros((amount,), jnp.int32).at[sequence[jnp.where(places < fixed, places, moved)]].set(jnp.asarray(sizes, jnp.int32))

    sizes = jnp.where(number % 4 == 0, named(heavy_load, number // 4), named(ordinary, number - number // 4 - 1))
    mixed = jax.random.permutation(jax.random.fold_in(own, 3), amount)
    donor, taker = mixed[0:amount // 2 * 2:2], mixed[1:amount // 2 * 2:2]
    room = jnp.minimum(sizes[donor] - 1, limit - sizes[taker]) // 2
    room = jnp.where((donor == sequence[0]) | (taker == sequence[0]) | (sizes[taker] == 0), 0, jnp.maximum(room, 0))
    moved = jax.random.randint(jax.random.fold_in(own, 4), (amount // 2,), 0, 1 << 20) % (room + 1)
    sizes = sizes.at[donor].add(-moved).at[taker].add(moved)
    labels = jnp.searchsorted(jnp.cumsum(sizes), jnp.arange(rows * top), side="right").astype(jnp.int32)
    grid = labels.reshape(top, rows).T
    grid = grid[jax.random.permutation(jax.random.fold_in(own, 1), rows)]
    offset_by = jax.random.randint(jax.random.fold_in(own, 2), (rows, 1), 0, top)
    return jnp.take_along_axis(grid, (jnp.arange(top)[None, :] + offset_by) % top, axis=1)


def shares(count, total, bound, lean, full):
    weights = [(1 << 20) // math.isqrt(standing ** lean) + 1 for standing in range(1, count + 1)]
    largest = bound if full else min(bound, max(-(-total // count), total * weights[0] // sum(weights)))
    least = 1 if total - largest >= count - 1 else 0
    given, rest = [largest] + [least] * (count - 1), total - largest - least * (count - 1)
    while rest > 0:
        free = [i for i in range(1, count) if given[i] < largest] or [i for i in range(1, count) if given[i] < bound]
        pool, budget = sum([weights[i] for i in free]), rest
        for i in free:
            more = min(bound - given[i], max(1, budget * weights[i] // pool), rest)
            given[i] = given[i] + more
            rest = rest - more
    return np.array(given)


def gaussian(rng, dims, spread, bound, split=(), kind=jnp.bfloat16):
    array = jax.random.normal(rng, dims, jnp.float32) * spread
    if len(split) > 0:
        array = levels(rng, dims, split, -0.22, 0.18) * array
    return jnp.clip(array, min=-bound, max=bound).astype(kind)


def setup_inputs(seed: int = 0) -> dict:
    keys = jax.random.split(jax.random.key(seed), 6)
    images = draw_images(jax.random.fold_in(keys[5], 71), 0)
    groups_keys = jax.random.split(jax.random.fold_in(keys[1], 1), PARTICLES // PART_DEV)
    groups_turns = jax.random.permutation(jax.random.fold_in(keys[1], 3), PARTICLES // PART_DEV)
    groups = jax.vmap(lambda own, number: shared_out(jax.random.fold_in(keys[1], 2), own, number, PART_DEV, N_CLS, 1, CAP, 2))(groups_keys, groups_turns).reshape((PARTICLES, 1))
    references = gaussian(keys[2], (CLASSES, PIX), PIX ** -0.5, 0.046875, ((0, 64), (1, 4)))
    interp_index = draw_interp_index(jax.random.fold_in(keys[5], 71), 0)
    shell_index = draw_shell_index(jax.random.fold_in(keys[5], 71), 0)
    return {"images": images, "groups": groups, "references": references, "interp_index": interp_index, "shell_index": shell_index}


EPS_W = 1e-05
EPS_F = 1e-06

def slab_sum(values, targets):
    column_ids = jnp.arange(PIXQ, dtype=jnp.int32) % IMG
    placed = targets + 2 * VBOX * PLANES * column_ids[None, :]
    return jax.ops.segment_sum(values.reshape(-1), placed.reshape(-1), num_segments=VOXS)

def owner_step(carry, inputs, images):
    slot_rows, owner_refs, owner_interp = inputs
    filled = slot_rows >= 0
    picked = jnp.take(images, jnp.maximum(slot_rows, 0), axis=0)
    picked = jnp.where(filled[:, None], picked, jnp.zeros((), images.dtype))
    rolled = jnp.concatenate([jnp.roll(owner_refs, -(shift_id - SHIFTS // 2), axis=2).reshape(CLS_DEV, PIX) for shift_id in range(SHIFTS)], axis=0)
    scores = jnp.dot(picked, rolled.T, preferred_element_type=jnp.float32)
    mean_square = lax.optimization_barrier(jnp.mean(scores * scores, axis=1, keepdims=True))
    weights = (scores * scores / (mean_square + EPS_W)).astype(jnp.bfloat16)
    summed = jnp.dot(weights.T, picked, preferred_element_type=jnp.float32).reshape(SHIFTS, CLS_DEV, IMG, IMG)
    aligned = jnp.roll(summed[0], -(SHIFTS // 2), axis=2)
    for shift_id in range(1, SHIFTS):
        aligned = aligned + jnp.roll(summed[shift_id], shift_id - SHIFTS // 2, axis=2)
    aligned = aligned.reshape(CLS_DEV, N_VOL, PIXQ)
    added = jax.vmap(slab_sum, in_axes=(1, 1))(aligned, owner_interp)
    return (carry + added, None)

def reference(images, groups, references, interp_index, shell_index):
    slot_total = N_CLS * CAP
    blocks = groups[:, 0].reshape(N_HALF * N_CLS, PART_DEV)
    matches = (blocks[:, :, None] == jnp.arange(N_CLS, dtype=jnp.int32)[None, None, :]).astype(jnp.int32)
    order_in = lax.optimization_barrier(jnp.sum(jnp.cumsum(matches, axis=1) * matches, axis=2)) - 1
    block_ids = jnp.arange(N_HALF * N_CLS, dtype=jnp.int32)
    halves = block_ids // N_CLS
    sources = block_ids % N_CLS
    target = (halves[:, None] * N_CLS + blocks) * slot_total + sources[:, None] * CAP + order_in
    table = jnp.full((N_HALF * N_CLS * slot_total,), -1, jnp.int32)
    table = table.at[target.reshape(-1).astype(jnp.int32)].set(jnp.arange(PARTICLES, dtype=jnp.int32))
    table = table.reshape(N_HALF, N_CLS, slot_total)
    grouped_refs = references.reshape(N_CLS, CLS_DEV, IMG, IMG)
    grouped_interp = interp_index.reshape(N_CLS, CLS_DEV, N_VOL, PIXQ)
    maps = []
    for half_id in range(N_HALF):
        start = jnp.zeros((N_VOL, VOXS), jnp.float32)
        half_map, _ = lax.scan(lambda carry, inputs: owner_step(carry, inputs, images), start, (table[half_id], grouped_refs, grouped_interp))
        maps.append(half_map)
    first, second = (maps[0], maps[1])
    flat_shells = shell_index.reshape(-1)
    sq_first = jax.ops.segment_sum((first * first).reshape(-1), flat_shells, num_segments=NSHELL)
    sq_second = jax.ops.segment_sum((second * second).reshape(-1), flat_shells, num_segments=NSHELL)
    cross = jax.ops.segment_sum((first * second).reshape(-1), flat_shells, num_segments=NSHELL)
    shell_fsc = cross / (jnp.sqrt(sq_first) * jnp.sqrt(sq_second) + EPS_F)
    mean_sq = (jnp.sum(sq_first) + jnp.sum(sq_second) + 2.0 * jnp.sum(cross)) / (4.0 * N_VOL * VOXS)
    volume = jnp.take(shell_fsc, shell_index) * (0.5 * (first + second)) / jnp.sqrt(mean_sq + EPS_F)
    return (volume, shell_fsc)
```

```python
import functools

import jax
import jax.numpy as jnp
from jax import lax
from jax.experimental import pallas as pl
from jax.experimental.pallas import tpu as pltpu
from jax.sharding import PartitionSpec as P

IMG = 128
SHIFTS = 5
NSHELL = 128
PLANES = 4
VBOX = 256
VOXS = 262144


EPS_W = 1e-05
EPS_F = 1e-06

LO = 128
Q_BLOCK = 16


def partner(shard, axis, apart):
    return lax.ppermute(shard, axis, [(i, i ^ 1 << apart) for i in range(lax.axis_size(axis))])


def _project_kernel(val_ref, idx_ref, out_ref):
    n = val_ref.shape[1]
    hi_count = out_ref.shape[1]
    lo_iota = lax.broadcasted_iota(jnp.int32, (LO, n), 0)
    hi_iota = lax.broadcasted_iota(jnp.int32, (hi_count, n), 0)

    def body(q, carry):
        v = val_ref[pl.ds(q, 1), :]
        idx = idx_ref[pl.ds(q, 1), :]
        lo = jnp.bitwise_and(idx, LO - 1)
        hi = jnp.right_shift(idx, 7)
        rt = jnp.where(lo == lo_iota, 1.0, 0.0).astype(jnp.bfloat16)
        vh = v.astype(jnp.bfloat16)
        vl = (v - vh.astype(jnp.float32)).astype(jnp.bfloat16)
        mask = hi == hi_iota
        zero = jnp.zeros((), jnp.bfloat16)
        lt = jnp.concatenate([jnp.where(mask, vh, zero), jnp.where(mask, vl, zero)], axis=0)
        o = lax.dot_general(lt, rt, (((1,), (1,)), ((), ())), preferred_element_type=jnp.float32)
        out_ref[q] = o[:hi_count] + o[hi_count:]
        return carry

    lax.fori_loop(0, val_ref.shape[0], body, 0)


def project(val_t, idx_t, bins):
    q_count, n = val_t.shape
    hi_count = bins // LO
    return pl.pallas_call(
        _project_kernel,
        out_shape=jax.ShapeDtypeStruct((q_count, hi_count, LO), jnp.float32),
        grid=(q_count // Q_BLOCK,),
        in_specs=[
            pl.BlockSpec((Q_BLOCK, n), lambda i: (i, 0)),
            pl.BlockSpec((Q_BLOCK, n), lambda i: (i, 0)),
        ],
        out_specs=pl.BlockSpec((Q_BLOCK, hi_count, LO), lambda i: (i, 0, 0)),
        cost_estimate=pl.CostEstimate(
            flops=2 * q_count * 2 * hi_count * LO * n,
            bytes_accessed=q_count * n * 8 + q_count * bins * 4,
            transcendentals=0,
        ),
    )(val_t, idx_t)


def shards(images, groups, references, interp_index, shell_index):
    n_cls = lax.axis_size("cls")
    n_vol = lax.axis_size("vol")
    n_half = lax.axis_size("half")
    part_count, pix_quarter = images.shape
    class_count = references.shape[0]
    capacity = max(2 * part_count // n_cls, 4)
    slot_count = n_cls * capacity
    owner_ids = groups[:, 0]
    matches = (owner_ids[:, None] == jnp.arange(n_cls, dtype=jnp.int32)[None, :]).astype(jnp.int32)
    order_in = jnp.sum(jnp.cumsum(matches, axis=0) * matches, axis=1) - 1
    slot_ids = owner_ids * capacity + order_in
    slot_hits = slot_ids[None, :] == jnp.arange(slot_count, dtype=jnp.int32)[:, None]
    source_ids = jnp.sum(
        jnp.where(slot_hits, jnp.arange(part_count, dtype=jnp.int32)[None, :], 0), axis=1
    )
    filled = jnp.any(slot_hits, axis=1)
    outgoing = jnp.where(
        filled[:, None], jnp.take(images, source_ids, axis=0), jnp.zeros((), jnp.bfloat16)
    )
    arrived = lax.all_to_all(
        outgoing.reshape(n_cls, capacity, pix_quarter),
        "cls",
        split_axis=0,
        concat_axis=0,
        tiled=True,
    )
    arrived = arrived.reshape(slot_count, pix_quarter)
    quarter_rows = pix_quarter // IMG
    bins = VOXS // IMG
    piece_rows = IMG // n_half
    idx_t = interp_index.reshape(class_count * quarter_rows, IMG).T
    idx_t = idx_t.reshape(n_half, piece_rows, -1).transpose(1, 0, 2).reshape(IMG, -1)
    shaped_refs = references.reshape(class_count, quarter_rows, IMG)
    rolled_refs = jnp.concatenate(
        [
            jnp.roll(shaped_refs, -(shift_id - SHIFTS // 2), axis=2).reshape(
                class_count, pix_quarter
            )
            for shift_id in range(SHIFTS)
        ],
        axis=0,
    )
    partial_scores = lax.dot_general(
        arrived, rolled_refs, (((1,), (1,)), ((), ())), preferred_element_type=jnp.float32
    )
    partial_scores = partial_scores.reshape(slot_count, SHIFTS, class_count)
    scores = lax.psum(partial_scores, "vol")
    squares = scores * scores
    mean_square = jnp.mean(squares, axis=(1, 2), keepdims=True)
    weights = (squares / (mean_square + EPS_W)).astype(jnp.bfloat16)
    weighted = lax.dot_general(
        weights.reshape(slot_count, SHIFTS * class_count),
        arrived,
        (((0,), (0,)), ((), ())),
        preferred_element_type=jnp.float32,
    )
    weighted = weighted.reshape(SHIFTS, class_count, quarter_rows, IMG)
    aligned = jnp.roll(weighted[0], -(SHIFTS // 2), axis=2)
    for shift_id in range(1, SHIFTS):
        aligned = aligned + jnp.roll(weighted[shift_id], shift_id - SHIFTS // 2, axis=2)
    val_t = aligned.reshape(class_count * quarter_rows, IMG).T
    val_t = val_t.reshape(n_half, piece_rows, -1).transpose(1, 0, 2).reshape(IMG, -1)
    slab_part = project(val_t, idx_t, bins)
    piece_len = VOXS // (n_half * n_cls)
    slab_part = slab_part.reshape(n_cls, n_half * piece_len)
    own_block = lax.psum_scatter(slab_part, "cls", scatter_dimension=0, tiled=True)
    own_block = own_block.reshape(n_half, piece_len)
    half_id = lax.axis_index("half")
    own_piece = jnp.where(half_id == 0, own_block[0], own_block[1])
    other_piece = jnp.where(half_id == 0, own_block[1], own_block[0])
    mirror_piece = partner(other_piece, "half", 0)
    first = jnp.where(half_id == 0, own_piece, mirror_piece)
    second = jnp.where(half_id == 0, mirror_piece, own_piece)
    shell_hot = (shell_index[0][:, None] == jnp.arange(NSHELL, dtype=jnp.int32)[None, :]).astype(
        jnp.float32
    )
    stats = jnp.stack([first * first, second * second, first * second])
    shell_terms = jnp.dot(stats, shell_hot, precision=lax.Precision.HIGHEST)
    shell_sums = lax.psum(shell_terms, ("half", "cls", "vol"))
    shell_fsc = shell_sums[2] / (jnp.sqrt(shell_sums[0]) * jnp.sqrt(shell_sums[1]) + EPS_F)
    mean_sq = (jnp.sum(shell_sums[0]) + jnp.sum(shell_sums[1]) + 2.0 * jnp.sum(shell_sums[2])) / (
        4.0 * n_vol * VOXS
    )
    filter_vox = jnp.dot(shell_hot, shell_fsc, precision=lax.Precision.HIGHEST)
    volume = filter_vox * (0.5 * (first + second)) / jnp.sqrt(mean_sq + EPS_F)
    return (volume[None, :], shell_fsc)


def solution(mesh):
    placed = (
        P(("half", "cls"), "vol"),
        P(("half", "cls"), None),
        P("cls", "vol"),
        P("cls", "vol"),
        P("vol", ("half", "cls")),
    )
    return jax.shard_map(
        shards,
        mesh=mesh,
        in_specs=placed,
        out_specs=(P("vol", ("half", "cls")), P()),
        check_vma=False,
    )
```

```python
import functools

import jax
import jax.numpy as jnp
from jax import lax
from jax.experimental import pallas as pl
from jax.experimental.pallas import tpu as pltpu
from jax.sharding import PartitionSpec as P

IMG = 128
SHIFTS = 5
NSHELL = 128
PLANES = 4
VBOX = 256
VOXS = 262144


EPS_W = 1e-05
EPS_F = 1e-06

LO = 128
Q_BLOCK = 16


def partner(shard, axis, apart):
    return lax.ppermute(shard, axis, [(i, i ^ 1 << apart) for i in range(lax.axis_size(axis))])


def butterfly_sum(x, axis):
    for bit in range(lax.axis_size(axis).bit_length() - 1):
        x = x + partner(x, axis, bit)
    return x


def halving_order(bits):
    if bits == 6:
        return [0, 2, 1, 3, 4, 5]
    return list(range(bits))


def reduce_scatter(x, axis):
    n = lax.axis_size(axis)
    bits = n.bit_length() - 1
    me = lax.axis_index(axis)
    remaining = list(range(bits - 1, -1, -1))
    data = x.reshape([2] * bits + [x.shape[1]])
    for bit in halving_order(bits):
        ax = remaining.index(bit)
        mine = jnp.right_shift(me, bit) & 1
        keep = lax.dynamic_index_in_dim(data, mine, axis=ax, keepdims=False)
        send = lax.dynamic_index_in_dim(data, 1 - mine, axis=ax, keepdims=False)
        data = keep + partner(send, axis, bit)
        remaining.remove(bit)
    return data


def _project_kernel(val_ref, idx_ref, out_ref):
    n = val_ref.shape[1]
    hi_count = out_ref.shape[1]
    lo_iota = lax.broadcasted_iota(jnp.int32, (LO, n), 0)
    hi_iota = lax.broadcasted_iota(jnp.int32, (hi_count, n), 0)

    def body(q, carry):
        v = val_ref[pl.ds(q, 1), :]
        idx = idx_ref[pl.ds(q, 1), :]
        lo = jnp.bitwise_and(idx, LO - 1)
        hi = jnp.right_shift(idx, 7)
        rt = jnp.where(lo == lo_iota, 1.0, 0.0).astype(jnp.bfloat16)
        vh = v.astype(jnp.bfloat16)
        vl = (v - vh.astype(jnp.float32)).astype(jnp.bfloat16)
        mask = hi == hi_iota
        zero = jnp.zeros((), jnp.bfloat16)
        lt = jnp.concatenate([jnp.where(mask, vh, zero), jnp.where(mask, vl, zero)], axis=0)
        o = lax.dot_general(lt, rt, (((1,), (1,)), ((), ())), preferred_element_type=jnp.float32)
        out_ref[q] = o[:hi_count] + o[hi_count:]
        return carry

    lax.fori_loop(0, val_ref.shape[0], body, 0)


def project(val_t, idx_t, bins):
    q_count, n = val_t.shape
    hi_count = bins // LO
    return pl.pallas_call(
        _project_kernel,
        out_shape=jax.ShapeDtypeStruct((q_count, hi_count, LO), jnp.float32),
        grid=(q_count // Q_BLOCK,),
        in_specs=[
            pl.BlockSpec((Q_BLOCK, n), lambda i: (i, 0)),
            pl.BlockSpec((Q_BLOCK, n), lambda i: (i, 0)),
        ],
        out_specs=pl.BlockSpec((Q_BLOCK, hi_count, LO), lambda i: (i, 0, 0)),
        cost_estimate=pl.CostEstimate(
            flops=2 * q_count * 2 * hi_count * LO * n,
            bytes_accessed=q_count * n * 8 + q_count * bins * 4,
            transcendentals=0,
        ),
    )(val_t, idx_t)


def shards(images, groups, references, interp_index, shell_index):
    n_cls = lax.axis_size("cls")
    n_vol = lax.axis_size("vol")
    n_half = lax.axis_size("half")
    part_count, pix_quarter = images.shape
    class_count = references.shape[0]
    capacity = max(2 * part_count // n_cls, 4)
    slot_count = n_cls * capacity
    owner_ids = groups[:, 0]
    matches = (owner_ids[:, None] == jnp.arange(n_cls, dtype=jnp.int32)[None, :]).astype(jnp.int32)
    order_in = jnp.sum(jnp.cumsum(matches, axis=0) * matches, axis=1) - 1
    slot_ids = owner_ids * capacity + order_in
    slot_hits = slot_ids[None, :] == jnp.arange(slot_count, dtype=jnp.int32)[:, None]
    source_ids = jnp.sum(
        jnp.where(slot_hits, jnp.arange(part_count, dtype=jnp.int32)[None, :], 0), axis=1
    )
    filled = jnp.any(slot_hits, axis=1)
    outgoing = jnp.where(
        filled[:, None], jnp.take(images, source_ids, axis=0), jnp.zeros((), jnp.bfloat16)
    )
    arrived = lax.all_to_all(
        outgoing.reshape(n_cls, capacity, pix_quarter),
        "cls",
        split_axis=0,
        concat_axis=0,
        tiled=True,
    )
    arrived = arrived.reshape(slot_count, pix_quarter)
    quarter_rows = pix_quarter // IMG
    bins = VOXS // IMG
    piece_rows = IMG // n_half
    idx_t = interp_index.reshape(class_count * quarter_rows, IMG).T
    idx_t = idx_t.reshape(n_half, piece_rows, -1).transpose(1, 0, 2).reshape(IMG, -1)
    shaped_refs = references.reshape(class_count, quarter_rows, IMG)
    rolled_refs = jnp.concatenate(
        [
            jnp.roll(shaped_refs, -(shift_id - SHIFTS // 2), axis=2).reshape(
                class_count, pix_quarter
            )
            for shift_id in range(SHIFTS)
        ],
        axis=0,
    )
    partial_scores = lax.dot_general(
        arrived, rolled_refs, (((1,), (1,)), ((), ())), preferred_element_type=jnp.float32
    )
    partial_scores = partial_scores.reshape(slot_count, SHIFTS, class_count)
    scores = butterfly_sum(partial_scores, "vol")
    squares = scores * scores
    mean_square = jnp.mean(squares, axis=(1, 2), keepdims=True)
    weights = (squares / (mean_square + EPS_W)).astype(jnp.bfloat16)
    weighted = lax.dot_general(
        weights.reshape(slot_count, SHIFTS * class_count),
        arrived,
        (((0,), (0,)), ((), ())),
        preferred_element_type=jnp.float32,
    )
    weighted = weighted.reshape(SHIFTS, class_count, quarter_rows, IMG)
    aligned = jnp.roll(weighted[0], -(SHIFTS // 2), axis=2)
    for shift_id in range(1, SHIFTS):
        aligned = aligned + jnp.roll(weighted[shift_id], shift_id - SHIFTS // 2, axis=2)
    val_t = aligned.reshape(class_count * quarter_rows, IMG).T
    val_t = val_t.reshape(n_half, piece_rows, -1).transpose(1, 0, 2).reshape(IMG, -1)
    slab_part = project(val_t, idx_t, bins)
    piece_len = VOXS // (n_half * n_cls)
    slab_part = slab_part.reshape(n_cls, n_half * piece_len)
    own_block = reduce_scatter(slab_part, "cls")
    own_block = own_block.reshape(n_half, piece_len)
    half_id = lax.axis_index("half")
    own_piece = jnp.where(half_id == 0, own_block[0], own_block[1])
    other_piece = jnp.where(half_id == 0, own_block[1], own_block[0])
    mirror_piece = partner(other_piece, "half", 0)
    first = jnp.where(half_id == 0, own_piece, mirror_piece)
    second = jnp.where(half_id == 0, mirror_piece, own_piece)
    shell_hot = (shell_index[0][:, None] == jnp.arange(NSHELL, dtype=jnp.int32)[None, :]).astype(
        jnp.float32
    )
    stats = jnp.stack([first * first, second * second, first * second])
    shell_terms = jnp.dot(stats, shell_hot, precision=lax.Precision.HIGHEST)
    shell_sums = butterfly_sum(butterfly_sum(butterfly_sum(shell_terms, "half"), "vol"), "cls")
    shell_fsc = shell_sums[2] / (jnp.sqrt(shell_sums[0]) * jnp.sqrt(shell_sums[1]) + EPS_F)
    mean_sq = (jnp.sum(shell_sums[0]) + jnp.sum(shell_sums[1]) + 2.0 * jnp.sum(shell_sums[2])) / (
        4.0 * n_vol * VOXS
    )
    filter_vox = jnp.dot(shell_hot, shell_fsc, precision=lax.Precision.HIGHEST)
    volume = filter_vox * (0.5 * (first + second)) / jnp.sqrt(mean_sq + EPS_F)
    return (volume[None, :], shell_fsc)


def solution(mesh):
    placed = (
        P(("half", "cls"), "vol"),
        P(("half", "cls"), None),
        P("cls", "vol"),
        P("cls", "vol"),
        P("vol", ("half", "cls")),
    )
    return jax.shard_map(
        shards,
        mesh=mesh,
        in_specs=placed,
        out_specs=(P("vol", ("half", "cls")), P()),
        check_vma=False,
    )
```

```python
import functools

import jax
import jax.numpy as jnp
from jax import lax
from jax.experimental import pallas as pl
from jax.experimental.pallas import tpu as pltpu
from jax.sharding import PartitionSpec as P

IMG = 128
SHIFTS = 5
NSHELL = 128
PLANES = 4
VBOX = 256
VOXS = 262144


EPS_W = 1e-05
EPS_F = 1e-06

LO = 128
Q_BLOCK = 16


def partner(shard, axis, apart):
    return lax.ppermute(shard, axis, [(i, i ^ 1 << apart) for i in range(lax.axis_size(axis))])


def digits_of(n):
    out, stride = [], 1
    while n % 4 == 0 and n > 1:
        out.append((stride, 4))
        stride, n = stride * 4, n // 4
    while n % 2 == 0 and n > 1:
        out.append((stride, 2))
        stride, n = stride * 2, n // 2
    return out


def shift_in_digit(x, axis, stride, radix, shift):
    n = lax.axis_size(axis)
    perm = []
    for i in range(n):
        d = (i // stride) % radix
        perm.append((i, i + ((d + shift) % radix - d) * stride))
    return lax.ppermute(x, axis, perm)


def digit_sum(x, axis):
    me = lax.axis_index(axis)
    for stride, radix in digits_of(lax.axis_size(axis)):
        d = (me // stride) % radix
        got = jnp.stack([x] + [shift_in_digit(x, axis, stride, radix, s) for s in range(1, radix)])
        total = lax.dynamic_index_in_dim(got, d % radix, keepdims=False)
        for t in range(1, radix):
            total = total + lax.dynamic_index_in_dim(got, (d - t) % radix, keepdims=False)
        x = total
    return x


def reduce_scatter(x, axis):
    me = lax.axis_index(axis)
    data = x
    for stride, radix in digits_of(lax.axis_size(axis)):
        d = (me // stride) % radix
        data = data.reshape(data.shape[0] // radix, radix, data.shape[1])
        total = lax.dynamic_index_in_dim(data, d, axis=1, keepdims=False)
        for s in range(1, radix):
            send = lax.dynamic_index_in_dim(data, (d + s) % radix, axis=1, keepdims=False)
            total = total + shift_in_digit(send, axis, stride, radix, s)
        data = total
    return data[0]


def _project_kernel(val_ref, idx_ref, out_ref):
    n = val_ref.shape[1]
    hi_count = out_ref.shape[1]
    lo_iota = lax.broadcasted_iota(jnp.int32, (LO, n), 0)
    hi_iota = lax.broadcasted_iota(jnp.int32, (hi_count, n), 0)

    def body(q, carry):
        v = val_ref[pl.ds(q, 1), :]
        idx = idx_ref[pl.ds(q, 1), :]
        lo = jnp.bitwise_and(idx, LO - 1)
        hi = jnp.right_shift(idx, 7)
        rt = jnp.where(lo == lo_iota, 1.0, 0.0).astype(jnp.bfloat16)
        vh = v.astype(jnp.bfloat16)
        vl = (v - vh.astype(jnp.float32)).astype(jnp.bfloat16)
        mask = hi == hi_iota
        zero = jnp.zeros((), jnp.bfloat16)
        lt = jnp.concatenate([jnp.where(mask, vh, zero), jnp.where(mask, vl, zero)], axis=0)
        o = lax.dot_general(lt, rt, (((1,), (1,)), ((), ())), preferred_element_type=jnp.float32)
        out_ref[q] = o[:hi_count] + o[hi_count:]
        return carry

    lax.fori_loop(0, val_ref.shape[0], body, 0)


def project(val_t, idx_t, bins):
    q_count, n = val_t.shape
    hi_count = bins // LO
    return pl.pallas_call(
        _project_kernel,
        out_shape=jax.ShapeDtypeStruct((q_count, hi_count, LO), jnp.float32),
        grid=(q_count // Q_BLOCK,),
        in_specs=[
            pl.BlockSpec((Q_BLOCK, n), lambda i: (i, 0)),
            pl.BlockSpec((Q_BLOCK, n), lambda i: (i, 0)),
        ],
        out_specs=pl.BlockSpec((Q_BLOCK, hi_count, LO), lambda i: (i, 0, 0)),
        cost_estimate=pl.CostEstimate(
            flops=2 * q_count * 2 * hi_count * LO * n,
            bytes_accessed=q_count * n * 8 + q_count * bins * 4,
            transcendentals=0,
        ),
    )(val_t, idx_t)


def shards(images, groups, references, interp_index, shell_index):
    n_cls = lax.axis_size("cls")
    n_vol = lax.axis_size("vol")
    n_half = lax.axis_size("half")
    part_count, pix_quarter = images.shape
    class_count = references.shape[0]
    capacity = max(2 * part_count // n_cls, 4)
    slot_count = n_cls * capacity
    owner_ids = groups[:, 0]
    matches = (owner_ids[:, None] == jnp.arange(n_cls, dtype=jnp.int32)[None, :]).astype(jnp.int32)
    order_in = jnp.sum(jnp.cumsum(matches, axis=0) * matches, axis=1) - 1
    slot_ids = owner_ids * capacity + order_in
    slot_hits = slot_ids[None, :] == jnp.arange(slot_count, dtype=jnp.int32)[:, None]
    source_ids = jnp.sum(
        jnp.where(slot_hits, jnp.arange(part_count, dtype=jnp.int32)[None, :], 0), axis=1
    )
    filled = jnp.any(slot_hits, axis=1)
    outgoing = jnp.where(
        filled[:, None], jnp.take(images, source_ids, axis=0), jnp.zeros((), jnp.bfloat16)
    )
    arrived = lax.all_to_all(
        outgoing.reshape(n_cls, capacity, pix_quarter),
        "cls",
        split_axis=0,
        concat_axis=0,
        tiled=True,
    )
    arrived = arrived.reshape(slot_count, pix_quarter)
    quarter_rows = pix_quarter // IMG
    bins = VOXS // IMG
    piece_rows = IMG // n_half
    idx_t = interp_index.reshape(class_count * quarter_rows, IMG).T
    idx_t = idx_t.reshape(n_half, piece_rows, -1).transpose(1, 0, 2).reshape(IMG, -1)
    shaped_refs = references.reshape(class_count, quarter_rows, IMG)
    rolled_refs = jnp.concatenate(
        [
            jnp.roll(shaped_refs, -(shift_id - SHIFTS // 2), axis=2).reshape(
                class_count, pix_quarter
            )
            for shift_id in range(SHIFTS)
        ],
        axis=0,
    )
    partial_scores = lax.dot_general(
        arrived, rolled_refs, (((1,), (1,)), ((), ())), preferred_element_type=jnp.float32
    )
    partial_scores = partial_scores.reshape(slot_count, SHIFTS, class_count)
    scores = digit_sum(partial_scores, "vol")
    squares = scores * scores
    mean_square = jnp.mean(squares, axis=(1, 2), keepdims=True)
    weights = (squares / (mean_square + EPS_W)).astype(jnp.bfloat16)
    weighted = lax.dot_general(
        weights.reshape(slot_count, SHIFTS * class_count),
        arrived,
        (((0,), (0,)), ((), ())),
        preferred_element_type=jnp.float32,
    )
    weighted = weighted.reshape(SHIFTS, class_count, quarter_rows, IMG)
    aligned = jnp.roll(weighted[0], -(SHIFTS // 2), axis=2)
    for shift_id in range(1, SHIFTS):
        aligned = aligned + jnp.roll(weighted[shift_id], shift_id - SHIFTS // 2, axis=2)
    val_t = aligned.reshape(class_count * quarter_rows, IMG).T
    val_t = val_t.reshape(n_half, piece_rows, -1).transpose(1, 0, 2).reshape(IMG, -1)
    slab_part = project(val_t, idx_t, bins)
    piece_len = VOXS // (n_half * n_cls)
    slab_part = slab_part.reshape(n_cls, n_half * piece_len)
    own_block = reduce_scatter(slab_part, "cls")
    half_id = lax.axis_index("half")
    other_block = partner(own_block, "half", 0)
    other_shell = partner(shell_index[0], "half", 0)
    first_block = jnp.where(half_id == 0, own_block, other_block)
    second_block = jnp.where(half_id == 0, other_block, own_block)
    shell_block = jnp.where(
        half_id == 0,
        jnp.concatenate([shell_index[0], other_shell]),
        jnp.concatenate([other_shell, shell_index[0]]),
    )
    block_hot = (shell_block[:, None] == jnp.arange(NSHELL, dtype=jnp.int32)[None, :]).astype(
        jnp.float32
    )
    stats = jnp.stack([first_block * first_block, second_block * second_block, first_block * second_block])
    shell_terms = jnp.dot(stats, block_hot, precision=lax.Precision.HIGHEST)
    shell_sums = digit_sum(digit_sum(shell_terms, "vol"), "cls")
    shell_fsc = shell_sums[2] / (jnp.sqrt(shell_sums[0]) * jnp.sqrt(shell_sums[1]) + EPS_F)
    mean_sq = (jnp.sum(shell_sums[0]) + jnp.sum(shell_sums[1]) + 2.0 * jnp.sum(shell_sums[2])) / (
        4.0 * n_vol * VOXS
    )
    first = lax.dynamic_index_in_dim(first_block.reshape(n_half, piece_len), half_id, keepdims=False)
    second = lax.dynamic_index_in_dim(second_block.reshape(n_half, piece_len), half_id, keepdims=False)
    shell_hot = (shell_index[0][:, None] == jnp.arange(NSHELL, dtype=jnp.int32)[None, :]).astype(
        jnp.float32
    )
    filter_vox = jnp.dot(shell_hot, shell_fsc, precision=lax.Precision.HIGHEST)
    volume = filter_vox * (0.5 * (first + second)) / jnp.sqrt(mean_sq + EPS_F)
    return (volume[None, :], shell_fsc)


def solution(mesh):
    placed = (
        P(("half", "cls"), "vol"),
        P(("half", "cls"), None),
        P("cls", "vol"),
        P("cls", "vol"),
        P("vol", ("half", "cls")),
    )
    return jax.shard_map(
        shards,
        mesh=mesh,
        in_specs=placed,
        out_specs=(P("vol", ("half", "cls")), P()),
        check_vma=False,
    )
```

```python
import functools

import jax
import jax.numpy as jnp
from jax import lax
from jax.experimental import pallas as pl
from jax.experimental.pallas import tpu as pltpu
from jax.sharding import PartitionSpec as P

IMG = 128
SHIFTS = 5
NSHELL = 128
PLANES = 4
VBOX = 256
VOXS = 262144


EPS_W = 1e-05
EPS_F = 1e-06

LO = 128


def partner(shard, axis, apart):
    return lax.ppermute(shard, axis, [(i, i ^ 1 << apart) for i in range(lax.axis_size(axis))])


def digits_of(n):
    out, stride = [], 1
    while n % 4 == 0 and n > 1:
        out.append((stride, 4))
        stride, n = stride * 4, n // 4
    while n % 2 == 0 and n > 1:
        out.append((stride, 2))
        stride, n = stride * 2, n // 2
    return out


def shift_in_digit(x, axis, stride, radix, shift):
    n = lax.axis_size(axis)
    perm = []
    for i in range(n):
        d = (i // stride) % radix
        perm.append((i, i + ((d + shift) % radix - d) * stride))
    return lax.ppermute(x, axis, perm)


def butterfly_sum(x, axis):
    for bit in range(lax.axis_size(axis).bit_length() - 1):
        x = x + partner(x, axis, bit)
    return x


def digit_sum(x, axis):
    me = lax.axis_index(axis)
    for stride, radix in digits_of(lax.axis_size(axis)):
        d = (me // stride) % radix
        got = jnp.stack([x] + [shift_in_digit(x, axis, stride, radix, s) for s in range(1, radix)])
        total = lax.dynamic_index_in_dim(got, d % radix, keepdims=False)
        for t in range(1, radix):
            total = total + lax.dynamic_index_in_dim(got, (d - t) % radix, keepdims=False)
        x = total
    return x


def reduce_scatter(x, axis):
    me = lax.axis_index(axis)
    data = x
    for stride, radix in digits_of(lax.axis_size(axis)):
        d = (me // stride) % radix
        data = data.reshape(data.shape[0], data.shape[1] // radix, radix, data.shape[2])
        total = lax.dynamic_index_in_dim(data, d, axis=2, keepdims=False)
        for s in range(1, radix):
            send = lax.dynamic_index_in_dim(data, (d + s) % radix, axis=2, keepdims=False)
            total = total + shift_in_digit(send, axis, stride, radix, s)
        data = total
    return data[:, 0]


def _project_kernel(val_ref, idx_ref, out_ref, vt_ref, it_ref):
    n = val_ref.shape[0]
    hi_count = out_ref.shape[1]
    vt_ref[...] = val_ref[...].T
    it_ref[...] = idx_ref[...].T
    lo_iota = lax.broadcasted_iota(jnp.int32, (LO, n), 0)
    hi_iota = lax.broadcasted_iota(jnp.int32, (hi_count, n), 0)

    def body(q, carry):
        v = vt_ref[pl.ds(q, 1), :]
        idx = it_ref[pl.ds(q, 1), :]
        lo = jnp.bitwise_and(idx, LO - 1)
        hi = jnp.right_shift(idx, 7)
        rt = jnp.where(lo == lo_iota, 1.0, 0.0).astype(jnp.bfloat16)
        vh = v.astype(jnp.bfloat16)
        vl = (v - vh.astype(jnp.float32)).astype(jnp.bfloat16)
        mask = hi == hi_iota
        zero = jnp.zeros((), jnp.bfloat16)
        lt = jnp.concatenate([jnp.where(mask, vh, zero), jnp.where(mask, vl, zero)], axis=0)
        o = lax.dot_general(lt, rt, (((1,), (1,)), ((), ())), preferred_element_type=jnp.float32)
        out_ref[q] = o[:hi_count] + o[hi_count:]
        return carry

    lax.fori_loop(0, IMG, body, 0)


def project(val, idx, bins):
    n, q_count = val.shape
    hi_count = bins // LO
    return pl.pallas_call(
        _project_kernel,
        out_shape=jax.ShapeDtypeStruct((q_count, hi_count, LO), jnp.float32),
        in_specs=[
            pl.BlockSpec(memory_space=pltpu.VMEM),
            pl.BlockSpec(memory_space=pltpu.VMEM),
        ],
        out_specs=pl.BlockSpec(memory_space=pltpu.VMEM),
        scratch_shapes=[
            pltpu.VMEM((q_count, n), jnp.float32),
            pltpu.VMEM((q_count, n), jnp.int32),
        ],
        cost_estimate=pl.CostEstimate(
            flops=2 * q_count * 2 * hi_count * LO * n,
            bytes_accessed=q_count * n * 8 + q_count * bins * 4,
            transcendentals=0,
        ),
    )(val, idx)


def shards(images, groups, references, interp_index, shell_index):
    n_cls = lax.axis_size("cls")
    n_vol = lax.axis_size("vol")
    n_half = lax.axis_size("half")
    part_count, pix_quarter = images.shape
    class_count = references.shape[0]
    capacity = max(2 * part_count // n_cls, 4)
    slot_count = n_cls * capacity
    owner_ids = groups[:, 0]
    matches = (owner_ids[:, None] == jnp.arange(n_cls, dtype=jnp.int32)[None, :]).astype(jnp.int32)
    order_in = jnp.sum(jnp.cumsum(matches, axis=0) * matches, axis=1) - 1
    slot_ids = owner_ids * capacity + order_in
    slot_hits = slot_ids[None, :] == jnp.arange(slot_count, dtype=jnp.int32)[:, None]
    source_ids = jnp.sum(
        jnp.where(slot_hits, jnp.arange(part_count, dtype=jnp.int32)[None, :], 0), axis=1
    )
    filled = jnp.any(slot_hits, axis=1)
    outgoing = jnp.where(
        filled[:, None], jnp.take(images, source_ids, axis=0), jnp.zeros((), jnp.bfloat16)
    )
    arrived = lax.all_to_all(outgoing, "cls", split_axis=0, concat_axis=0, tiled=True)
    quarter_rows = pix_quarter // IMG
    bins = VOXS // IMG
    shaped_refs = references.reshape(class_count, quarter_rows, IMG)
    rolled_refs = jnp.concatenate(
        [
            jnp.roll(shaped_refs, -(shift_id - SHIFTS // 2), axis=2).reshape(
                class_count, pix_quarter
            )
            for shift_id in range(SHIFTS)
        ],
        axis=0,
    )
    partial_scores = lax.dot_general(
        arrived, rolled_refs, (((1,), (1,)), ((), ())), preferred_element_type=jnp.float32
    )
    partial_scores = partial_scores.reshape(slot_count, SHIFTS, class_count)
    scores = digit_sum(partial_scores, "vol")
    squares = scores * scores
    mean_square = jnp.mean(squares, axis=(1, 2), keepdims=True)
    weights = (squares / (mean_square + EPS_W)).astype(jnp.bfloat16)
    weighted = lax.dot_general(
        weights.reshape(slot_count, SHIFTS * class_count),
        arrived,
        (((0,), (0,)), ((), ())),
        preferred_element_type=jnp.float32,
    )
    weighted = weighted.reshape(SHIFTS, class_count, quarter_rows, IMG)
    aligned = jnp.roll(weighted[0], -(SHIFTS // 2), axis=2)
    for shift_id in range(1, SHIFTS):
        aligned = aligned + jnp.roll(weighted[shift_id], shift_id - SHIFTS // 2, axis=2)
    slab_part = project(
        aligned.reshape(class_count * quarter_rows, IMG),
        interp_index.reshape(class_count * quarter_rows, IMG),
        bins,
    )
    piece_len = VOXS // (n_half * n_cls)
    slab_part = slab_part.reshape(n_half, n_cls, piece_len)
    own_block = reduce_scatter(slab_part, "cls").reshape(-1)
    half_id = lax.axis_index("half")
    other_block = partner(own_block, "half", 0)
    other_shell = partner(shell_index[0], "half", 0)
    first_block = jnp.where(half_id == 0, own_block, other_block)
    second_block = jnp.where(half_id == 0, other_block, own_block)
    shell_block = jnp.where(
        half_id == 0,
        jnp.concatenate([shell_index[0], other_shell]),
        jnp.concatenate([other_shell, shell_index[0]]),
    )
    block_hot = (shell_block[:, None] == jnp.arange(NSHELL, dtype=jnp.int32)[None, :]).astype(
        jnp.float32
    )
    stats = jnp.stack([first_block * first_block, second_block * second_block, first_block * second_block])
    shell_terms = jnp.dot(stats, block_hot, precision=lax.Precision.HIGHEST)
    shell_sums = butterfly_sum(butterfly_sum(shell_terms, "vol"), "cls")
    shell_fsc = shell_sums[2] / (jnp.sqrt(shell_sums[0]) * jnp.sqrt(shell_sums[1]) + EPS_F)
    mean_sq = (jnp.sum(shell_sums[0]) + jnp.sum(shell_sums[1]) + 2.0 * jnp.sum(shell_sums[2])) / (
        4.0 * n_vol * VOXS
    )
    first = lax.dynamic_index_in_dim(first_block.reshape(n_half, piece_len), half_id, keepdims=False)
    second = lax.dynamic_index_in_dim(second_block.reshape(n_half, piece_len), half_id, keepdims=False)
    shell_hot = (shell_index[0][:, None] == jnp.arange(NSHELL, dtype=jnp.int32)[None, :]).astype(
        jnp.float32
    )
    filter_vox = jnp.dot(shell_hot, shell_fsc, precision=lax.Precision.HIGHEST)
    volume = filter_vox * (0.5 * (first + second)) / jnp.sqrt(mean_sq + EPS_F)
    return (volume[None, :], shell_fsc)


def solution(mesh):
    placed = (
        P(("half", "cls"), "vol"),
        P(("half", "cls"), None),
        P("cls", "vol"),
        P("cls", "vol"),
        P("vol", ("half", "cls")),
    )
    return jax.shard_map(
        shards,
        mesh=mesh,
        in_specs=placed,
        out_specs=(P("vol", ("half", "cls")), P()),
        check_vma=False,
    )
```

```python
import functools

import jax
import jax.numpy as jnp
from jax import lax
from jax.experimental import pallas as pl
from jax.experimental.pallas import tpu as pltpu
from jax.sharding import PartitionSpec as P

IMG = 128
SHIFTS = 5
NSHELL = 128
PLANES = 4
VBOX = 256
VOXS = 262144


EPS_W = 1e-05
EPS_F = 1e-06

LO = 128


def partner(shard, axis, apart):
    return lax.ppermute(shard, axis, [(i, i ^ 1 << apart) for i in range(lax.axis_size(axis))])


def digits_of(n):
    out, stride = [], 1
    while n % 4 == 0 and n > 1:
        out.append((stride, 4))
        stride, n = stride * 4, n // 4
    while n % 2 == 0 and n > 1:
        out.append((stride, 2))
        stride, n = stride * 2, n // 2
    return out


def shift_in_digit(x, axis, stride, radix, shift):
    n = lax.axis_size(axis)
    perm = []
    for i in range(n):
        d = (i // stride) % radix
        perm.append((i, i + ((d + shift) % radix - d) * stride))
    return lax.ppermute(x, axis, perm)


def butterfly_sum(x, axis):
    for bit in range(lax.axis_size(axis).bit_length() - 1):
        x = x + partner(x, axis, bit)
    return x


def exchange_sum(x, axis):
    n = lax.axis_size(axis)
    got = lax.all_to_all(jnp.broadcast_to(x[None], (n,) + x.shape), axis, 0, 0, tiled=True)
    total = got[0]
    for i in range(1, n):
        total = total + got[i]
    return total


def digit_sum(x, axis):
    me = lax.axis_index(axis)
    for stride, radix in digits_of(lax.axis_size(axis)):
        d = (me // stride) % radix
        got = jnp.stack([x] + [shift_in_digit(x, axis, stride, radix, s) for s in range(1, radix)])
        total = lax.dynamic_index_in_dim(got, d % radix, keepdims=False)
        for t in range(1, radix):
            total = total + lax.dynamic_index_in_dim(got, (d - t) % radix, keepdims=False)
        x = total
    return x


def reduce_scatter(x, axis):
    me = lax.axis_index(axis)
    data = x
    for stride, radix in digits_of(lax.axis_size(axis)):
        d = (me // stride) % radix
        data = data.reshape(data.shape[0], data.shape[1] // radix, radix, data.shape[2])
        total = lax.dynamic_index_in_dim(data, d, axis=2, keepdims=False)
        for s in range(1, radix):
            send = lax.dynamic_index_in_dim(data, (d + s) % radix, axis=2, keepdims=False)
            total = total + shift_in_digit(send, axis, stride, radix, s)
        data = total
    return data[:, 0]


def _project_kernel(val_ref, idx_ref, out_ref, vt_ref, it_ref):
    n = val_ref.shape[0]
    hi_count = out_ref.shape[1]
    vt_ref[...] = val_ref[...].T
    it_ref[...] = idx_ref[...].T
    lo_iota = lax.broadcasted_iota(jnp.int32, (LO, n), 0)
    hi_iota = lax.broadcasted_iota(jnp.int32, (hi_count, n), 0)

    def body(q, carry):
        v = vt_ref[pl.ds(q, 1), :]
        idx = it_ref[pl.ds(q, 1), :]
        lo = jnp.bitwise_and(idx, LO - 1)
        hi = jnp.right_shift(idx, 7)
        rt = jnp.where(lo == lo_iota, 1.0, 0.0).astype(jnp.bfloat16)
        vh = v.astype(jnp.bfloat16)
        vl = (v - vh.astype(jnp.float32)).astype(jnp.bfloat16)
        mask = hi == hi_iota
        zero = jnp.zeros((), jnp.bfloat16)
        lt = jnp.concatenate([jnp.where(mask, vh, zero), jnp.where(mask, vl, zero)], axis=0)
        o = lax.dot_general(lt, rt, (((1,), (1,)), ((), ())), preferred_element_type=jnp.float32)
        out_ref[q] = o[:hi_count] + o[hi_count:]
        return carry

    lax.fori_loop(0, IMG, body, 0)


def project(val, idx, bins):
    n, q_count = val.shape
    hi_count = bins // LO
    return pl.pallas_call(
        _project_kernel,
        out_shape=jax.ShapeDtypeStruct((q_count, hi_count, LO), jnp.float32),
        in_specs=[
            pl.BlockSpec(memory_space=pltpu.VMEM),
            pl.BlockSpec(memory_space=pltpu.VMEM),
        ],
        out_specs=pl.BlockSpec(memory_space=pltpu.VMEM),
        scratch_shapes=[
            pltpu.VMEM((q_count, n), jnp.float32),
            pltpu.VMEM((q_count, n), jnp.int32),
        ],
        cost_estimate=pl.CostEstimate(
            flops=2 * q_count * 2 * hi_count * LO * n,
            bytes_accessed=q_count * n * 8 + q_count * bins * 4,
            transcendentals=0,
        ),
    )(val, idx)


def shards(images, groups, references, interp_index, shell_index):
    n_cls = lax.axis_size("cls")
    n_vol = lax.axis_size("vol")
    n_half = lax.axis_size("half")
    part_count, pix_quarter = images.shape
    class_count = references.shape[0]
    capacity = max(2 * part_count // n_cls, 4)
    slot_count = n_cls * capacity
    owner_ids = groups[:, 0]
    matches = (owner_ids[:, None] == jnp.arange(n_cls, dtype=jnp.int32)[None, :]).astype(jnp.int32)
    order_in = jnp.sum(jnp.cumsum(matches, axis=0) * matches, axis=1) - 1
    slot_ids = owner_ids * capacity + order_in
    slot_hits = slot_ids[None, :] == jnp.arange(slot_count, dtype=jnp.int32)[:, None]
    source_ids = jnp.sum(
        jnp.where(slot_hits, jnp.arange(part_count, dtype=jnp.int32)[None, :], 0), axis=1
    )
    filled = jnp.any(slot_hits, axis=1)
    outgoing = jnp.where(
        filled[:, None], jnp.take(images, source_ids, axis=0), jnp.zeros((), jnp.bfloat16)
    )
    arrived = lax.all_to_all(outgoing, "cls", split_axis=0, concat_axis=0, tiled=True)
    quarter_rows = pix_quarter // IMG
    bins = VOXS // IMG
    shaped_refs = references.reshape(class_count, quarter_rows, IMG)
    rolled_refs = jnp.concatenate(
        [
            jnp.roll(shaped_refs, -(shift_id - SHIFTS // 2), axis=2).reshape(
                class_count, pix_quarter
            )
            for shift_id in range(SHIFTS)
        ],
        axis=0,
    )
    partial_scores = lax.dot_general(
        arrived, rolled_refs, (((1,), (1,)), ((), ())), preferred_element_type=jnp.float32
    )
    partial_scores = partial_scores.reshape(slot_count, SHIFTS, class_count)
    scores = exchange_sum(partial_scores, "vol")
    squares = scores * scores
    mean_square = jnp.mean(squares, axis=(1, 2), keepdims=True)
    weights = (squares / (mean_square + EPS_W)).astype(jnp.bfloat16)
    weighted = lax.dot_general(
        weights.reshape(slot_count, SHIFTS * class_count),
        arrived,
        (((0,), (0,)), ((), ())),
        preferred_element_type=jnp.float32,
    )
    weighted = weighted.reshape(SHIFTS, class_count, quarter_rows, IMG)
    aligned = jnp.roll(weighted[0], -(SHIFTS // 2), axis=2)
    for shift_id in range(1, SHIFTS):
        aligned = aligned + jnp.roll(weighted[shift_id], shift_id - SHIFTS // 2, axis=2)
    slab_part = project(
        aligned.reshape(class_count * quarter_rows, IMG),
        interp_index.reshape(class_count * quarter_rows, IMG),
        bins,
    )
    piece_len = VOXS // (n_half * n_cls)
    slab_part = slab_part.reshape(n_half, n_cls, piece_len)
    own_block = reduce_scatter(slab_part, "cls").reshape(-1)
    half_id = lax.axis_index("half")
    other_block = partner(own_block, "half", 0)
    other_shell = partner(shell_index[0], "half", 0)
    first_block = jnp.where(half_id == 0, own_block, other_block)
    second_block = jnp.where(half_id == 0, other_block, own_block)
    shell_block = jnp.where(
        half_id == 0,
        jnp.concatenate([shell_index[0], other_shell]),
        jnp.concatenate([other_shell, shell_index[0]]),
    )
    block_hot = (shell_block[:, None] == jnp.arange(NSHELL, dtype=jnp.int32)[None, :]).astype(
        jnp.float32
    )
    stats = jnp.stack([first_block * first_block, second_block * second_block, first_block * second_block])
    shell_terms = jnp.dot(stats, block_hot, precision=lax.Precision.HIGHEST)
    shell_sums = exchange_sum(exchange_sum(shell_terms, "vol"), "cls")
    shell_fsc = shell_sums[2] / (jnp.sqrt(shell_sums[0]) * jnp.sqrt(shell_sums[1]) + EPS_F)
    mean_sq = (jnp.sum(shell_sums[0]) + jnp.sum(shell_sums[1]) + 2.0 * jnp.sum(shell_sums[2])) / (
        4.0 * n_vol * VOXS
    )
    first = lax.dynamic_index_in_dim(first_block.reshape(n_half, piece_len), half_id, keepdims=False)
    second = lax.dynamic_index_in_dim(second_block.reshape(n_half, piece_len), half_id, keepdims=False)
    shell_hot = (shell_index[0][:, None] == jnp.arange(NSHELL, dtype=jnp.int32)[None, :]).astype(
        jnp.float32
    )
    filter_vox = jnp.dot(shell_hot, shell_fsc, precision=lax.Precision.HIGHEST)
    volume = filter_vox * (0.5 * (first + second)) / jnp.sqrt(mean_sq + EPS_F)
    return (volume[None, :], shell_fsc)


def solution(mesh):
    placed = (
        P(("half", "cls"), "vol"),
        P(("half", "cls"), None),
        P("cls", "vol"),
        P("cls", "vol"),
        P("vol", ("half", "cls")),
    )
    return jax.shard_map(
        shards,
        mesh=mesh,
        in_specs=placed,
        out_specs=(P("vol", ("half", "cls")), P()),
        check_vma=False,
    )
```

```python
import functools

import jax
import jax.numpy as jnp
from jax import lax
from jax.experimental import pallas as pl
from jax.experimental.pallas import tpu as pltpu
from jax.sharding import PartitionSpec as P

IMG = 128
SHIFTS = 5
NSHELL = 128
PLANES = 4
VBOX = 256
VOXS = 262144


EPS_W = 1e-05
EPS_F = 1e-06

LO = 128


def partner(shard, axis, apart):
    return lax.ppermute(shard, axis, [(i, i ^ 1 << apart) for i in range(lax.axis_size(axis))])


def digits_of(n):
    out, stride = [], 1
    while n % 4 == 0 and n > 1:
        out.append((stride, 4))
        stride, n = stride * 4, n // 4
    while n % 2 == 0 and n > 1:
        out.append((stride, 2))
        stride, n = stride * 2, n // 2
    return out


def shift_in_digit(x, axis, stride, radix, shift):
    n = lax.axis_size(axis)
    perm = []
    for i in range(n):
        d = (i // stride) % radix
        perm.append((i, i + ((d + shift) % radix - d) * stride))
    return lax.ppermute(x, axis, perm)


def butterfly_sum(x, axis):
    for bit in range(lax.axis_size(axis).bit_length() - 1):
        x = x + partner(x, axis, bit)
    return x


def exchange_sum(x, axis):
    n = lax.axis_size(axis)
    got = lax.all_to_all(jnp.broadcast_to(x[None], (n,) + x.shape), axis, 0, 0, tiled=True)
    total = got[0]
    for i in range(1, n):
        total = total + got[i]
    return total


def digit_sum(x, axis):
    me = lax.axis_index(axis)
    for stride, radix in digits_of(lax.axis_size(axis)):
        d = (me // stride) % radix
        got = jnp.stack([x] + [shift_in_digit(x, axis, stride, radix, s) for s in range(1, radix)])
        total = lax.dynamic_index_in_dim(got, d % radix, keepdims=False)
        for t in range(1, radix):
            total = total + lax.dynamic_index_in_dim(got, (d - t) % radix, keepdims=False)
        x = total
    return x


def reduce_scatter(x, axis):
    me = lax.axis_index(axis)
    data = x
    for stride, radix in digits_of(lax.axis_size(axis)):
        d = (me // stride) % radix
        data = data.reshape(data.shape[0], data.shape[1] // radix, radix, data.shape[2])
        total = lax.dynamic_index_in_dim(data, d, axis=2, keepdims=False)
        for s in range(1, radix):
            send = lax.dynamic_index_in_dim(data, (d + s) % radix, axis=2, keepdims=False)
            total = total + shift_in_digit(send, axis, stride, radix, s)
        data = total
    return data[:, 0]


def _project_kernel(w_ref, idx_ref, out_ref, wt_ref, it_ref):
    n = idx_ref.shape[0]
    hi_count = out_ref.shape[1]
    for shift_id in range(SHIFTS):
        wt_ref[shift_id] = w_ref[shift_id].T
    it_ref[...] = idx_ref[...].T
    lo_iota = lax.broadcasted_iota(jnp.int32, (LO, n), 0)
    hi_iota = lax.broadcasted_iota(jnp.int32, (hi_count, n), 0)

    def body(q, carry):
        v = wt_ref[0, pl.ds(lax.rem(q + SHIFTS // 2, IMG), 1), :]
        for shift_id in range(1, SHIFTS):
            row = lax.rem(q - (shift_id - SHIFTS // 2) + IMG, IMG)
            v = v + wt_ref[shift_id, pl.ds(row, 1), :]
        idx = it_ref[pl.ds(q, 1), :]
        lo = jnp.bitwise_and(idx, LO - 1)
        hi = jnp.right_shift(idx, 7)
        rt = jnp.where(lo == lo_iota, 1.0, 0.0).astype(jnp.bfloat16)
        vh = v.astype(jnp.bfloat16)
        vl = (v - vh.astype(jnp.float32)).astype(jnp.bfloat16)
        mask = hi == hi_iota
        zero = jnp.zeros((), jnp.bfloat16)
        lt = jnp.concatenate([jnp.where(mask, vh, zero), jnp.where(mask, vl, zero)], axis=0)
        o = lax.dot_general(lt, rt, (((1,), (1,)), ((), ())), preferred_element_type=jnp.float32)
        out_ref[q] = o[:hi_count] + o[hi_count:]
        return carry

    lax.fori_loop(0, IMG, body, 0)


def project(weighted, idx, bins):
    n, q_count = idx.shape
    hi_count = bins // LO
    return pl.pallas_call(
        _project_kernel,
        out_shape=jax.ShapeDtypeStruct((q_count, hi_count, LO), jnp.float32),
        in_specs=[
            pl.BlockSpec(memory_space=pltpu.VMEM),
            pl.BlockSpec(memory_space=pltpu.VMEM),
        ],
        out_specs=pl.BlockSpec(memory_space=pltpu.VMEM),
        scratch_shapes=[
            pltpu.VMEM((SHIFTS, q_count, n), jnp.float32),
            pltpu.VMEM((q_count, n), jnp.int32),
        ],
        cost_estimate=pl.CostEstimate(
            flops=2 * q_count * 2 * hi_count * LO * n,
            bytes_accessed=q_count * n * (4 * SHIFTS + 4) + q_count * bins * 4,
            transcendentals=0,
        ),
    )(weighted, idx)


def shards(images, groups, references, interp_index, shell_index):
    n_cls = lax.axis_size("cls")
    n_vol = lax.axis_size("vol")
    n_half = lax.axis_size("half")
    part_count, pix_quarter = images.shape
    class_count = references.shape[0]
    capacity = max(2 * part_count // n_cls, 4)
    slot_count = n_cls * capacity
    owner_ids = groups[:, 0]
    matches = (owner_ids[:, None] == jnp.arange(n_cls, dtype=jnp.int32)[None, :]).astype(jnp.int32)
    order_in = jnp.sum(jnp.cumsum(matches, axis=0) * matches, axis=1) - 1
    slot_ids = owner_ids * capacity + order_in
    slot_hits = slot_ids[None, :] == jnp.arange(slot_count, dtype=jnp.int32)[:, None]
    outgoing = jnp.dot(
        slot_hits.astype(jnp.bfloat16), images, preferred_element_type=jnp.float32
    ).astype(jnp.bfloat16)
    arrived = lax.all_to_all(outgoing, "cls", split_axis=0, concat_axis=0, tiled=True)
    quarter_rows = pix_quarter // IMG
    bins = VOXS // IMG
    shaped_refs = references.reshape(class_count, quarter_rows, IMG)
    rolled_refs = jnp.concatenate(
        [
            jnp.roll(shaped_refs, -(shift_id - SHIFTS // 2), axis=2).reshape(
                class_count, pix_quarter
            )
            for shift_id in range(SHIFTS)
        ],
        axis=0,
    )
    partial_scores = lax.dot_general(
        arrived, rolled_refs, (((1,), (1,)), ((), ())), preferred_element_type=jnp.float32
    )
    partial_scores = partial_scores.reshape(slot_count, SHIFTS, class_count)
    scores = exchange_sum(partial_scores, "vol")
    squares = scores * scores
    mean_square = jnp.mean(squares, axis=(1, 2), keepdims=True)
    weights = (squares / (mean_square + EPS_W)).astype(jnp.bfloat16)
    weighted = lax.dot_general(
        weights.reshape(slot_count, SHIFTS * class_count),
        arrived,
        (((0,), (0,)), ((), ())),
        preferred_element_type=jnp.float32,
    )
    slab_part = project(
        weighted.reshape(SHIFTS, class_count * quarter_rows, IMG),
        interp_index.reshape(class_count * quarter_rows, IMG),
        bins,
    )
    piece_len = VOXS // (n_half * n_cls)
    slab_part = slab_part.reshape(n_half, n_cls, piece_len)
    own_block = reduce_scatter(slab_part, "cls").reshape(-1)
    half_id = lax.axis_index("half")
    other_block = partner(own_block, "half", 0)
    other_shell = partner(shell_index[0], "half", 0)
    first_block = jnp.where(half_id == 0, own_block, other_block)
    second_block = jnp.where(half_id == 0, other_block, own_block)
    shell_block = jnp.where(
        half_id == 0,
        jnp.concatenate([shell_index[0], other_shell]),
        jnp.concatenate([other_shell, shell_index[0]]),
    )
    block_hot = (shell_block[:, None] == jnp.arange(NSHELL, dtype=jnp.int32)[None, :]).astype(
        jnp.float32
    )
    stats = jnp.stack([first_block * first_block, second_block * second_block, first_block * second_block])
    shell_terms = jnp.dot(stats, block_hot, precision=lax.Precision.HIGHEST)
    shell_sums = exchange_sum(exchange_sum(shell_terms, "vol"), "cls")
    shell_fsc = shell_sums[2] / (jnp.sqrt(shell_sums[0]) * jnp.sqrt(shell_sums[1]) + EPS_F)
    mean_sq = (jnp.sum(shell_sums[0]) + jnp.sum(shell_sums[1]) + 2.0 * jnp.sum(shell_sums[2])) / (
        4.0 * n_vol * VOXS
    )
    first = lax.dynamic_index_in_dim(first_block.reshape(n_half, piece_len), half_id, keepdims=False)
    second = lax.dynamic_index_in_dim(second_block.reshape(n_half, piece_len), half_id, keepdims=False)
    shell_hot = (shell_index[0][:, None] == jnp.arange(NSHELL, dtype=jnp.int32)[None, :]).astype(
        jnp.float32
    )
    filter_vox = jnp.dot(shell_hot, shell_fsc, precision=lax.Precision.HIGHEST)
    volume = filter_vox * (0.5 * (first + second)) / jnp.sqrt(mean_sq + EPS_F)
    return (volume[None, :], shell_fsc)


def solution(mesh):
    placed = (
        P(("half", "cls"), "vol"),
        P(("half", "cls"), None),
        P("cls", "vol"),
        P("cls", "vol"),
        P("vol", ("half", "cls")),
    )
    return jax.shard_map(
        shards,
        mesh=mesh,
        in_specs=placed,
        out_specs=(P("vol", ("half", "cls")), P()),
        check_vma=False,
    )
```

```python
import functools

import jax
import jax.numpy as jnp
from jax import lax
from jax.experimental import pallas as pl
from jax.experimental.pallas import tpu as pltpu
from jax.sharding import PartitionSpec as P

IMG = 128
SHIFTS = 5
NSHELL = 128
PLANES = 4
VBOX = 256
VOXS = 262144


EPS_W = 1e-05
EPS_F = 1e-06

LO = 128


def partner(shard, axis, apart):
    return lax.ppermute(shard, axis, [(i, i ^ 1 << apart) for i in range(lax.axis_size(axis))])


def digits_of(n):
    out, stride = [], 1
    while n % 4 == 0 and n > 1:
        out.append((stride, 4))
        stride, n = stride * 4, n // 4
    while n % 2 == 0 and n > 1:
        out.append((stride, 2))
        stride, n = stride * 2, n // 2
    return out


def shift_in_digit(x, axis, stride, radix, shift):
    n = lax.axis_size(axis)
    perm = []
    for i in range(n):
        d = (i // stride) % radix
        perm.append((i, i + ((d + shift) % radix - d) * stride))
    return lax.ppermute(x, axis, perm)


def butterfly_sum(x, axis):
    for bit in range(lax.axis_size(axis).bit_length() - 1):
        x = x + partner(x, axis, bit)
    return x


def exchange_sum(x, axis):
    n = lax.axis_size(axis)
    got = lax.all_to_all(jnp.broadcast_to(x[None], (n,) + x.shape), axis, 0, 0, tiled=True)
    total = got[0]
    for i in range(1, n):
        total = total + got[i]
    return total


def digit_sum(x, axis):
    me = lax.axis_index(axis)
    for stride, radix in digits_of(lax.axis_size(axis)):
        d = (me // stride) % radix
        got = jnp.stack([x] + [shift_in_digit(x, axis, stride, radix, s) for s in range(1, radix)])
        total = lax.dynamic_index_in_dim(got, d % radix, keepdims=False)
        for t in range(1, radix):
            total = total + lax.dynamic_index_in_dim(got, (d - t) % radix, keepdims=False)
        x = total
    return x


def reduce_scatter(x, axis):
    me = lax.axis_index(axis)
    data = x
    for stride, radix in digits_of(lax.axis_size(axis)):
        d = (me // stride) % radix
        data = data.reshape(data.shape[0], data.shape[1] // radix, radix, data.shape[2])
        total = lax.dynamic_index_in_dim(data, d, axis=2, keepdims=False)
        for s in range(1, radix):
            send = lax.dynamic_index_in_dim(data, (d + s) % radix, axis=2, keepdims=False)
            total = total + shift_in_digit(send, axis, stride, radix, s)
        data = total
    return data[:, 0]


def _project_kernel(w_ref, idx_ref, out_ref, wt_ref, it_ref):
    n = idx_ref.shape[0]
    hi_count = out_ref.shape[1]
    for shift_id in range(SHIFTS):
        wt_ref[shift_id] = w_ref[shift_id].T
    it_ref[...] = idx_ref[...].T
    lo_iota = lax.broadcasted_iota(jnp.int32, (LO, n), 0)
    hi_iota = lax.broadcasted_iota(jnp.int32, (hi_count, n), 0)

    def body(q, carry):
        v = wt_ref[0, pl.ds(lax.rem(q + SHIFTS // 2, IMG), 1), :]
        for shift_id in range(1, SHIFTS):
            row = lax.rem(q - (shift_id - SHIFTS // 2) + IMG, IMG)
            v = v + wt_ref[shift_id, pl.ds(row, 1), :]
        idx = it_ref[pl.ds(q, 1), :]
        lo = jnp.bitwise_and(idx, LO - 1)
        hi = jnp.right_shift(idx, 7)
        rt = jnp.where(lo == lo_iota, 1.0, 0.0).astype(jnp.bfloat16)
        vh = v.astype(jnp.bfloat16)
        vl = (v - vh.astype(jnp.float32)).astype(jnp.bfloat16)
        mask = hi == hi_iota
        zero = jnp.zeros((), jnp.bfloat16)
        lt = jnp.concatenate([jnp.where(mask, vh, zero), jnp.where(mask, vl, zero)], axis=0)
        o = lax.dot_general(lt, rt, (((1,), (1,)), ((), ())), preferred_element_type=jnp.float32)
        out_ref[q] = o[:hi_count] + o[hi_count:]
        return carry

    lax.fori_loop(0, IMG, body, 0, unroll=16)


def project(weighted, idx, bins):
    n, q_count = idx.shape
    hi_count = bins // LO
    return pl.pallas_call(
        _project_kernel,
        out_shape=jax.ShapeDtypeStruct((q_count, hi_count, LO), jnp.float32),
        in_specs=[
            pl.BlockSpec(memory_space=pltpu.VMEM),
            pl.BlockSpec(memory_space=pltpu.VMEM),
        ],
        out_specs=pl.BlockSpec(memory_space=pltpu.VMEM),
        scratch_shapes=[
            pltpu.VMEM((SHIFTS, q_count, n), jnp.float32),
            pltpu.VMEM((q_count, n), jnp.int32),
        ],
        cost_estimate=pl.CostEstimate(
            flops=2 * q_count * 2 * hi_count * LO * n,
            bytes_accessed=q_count * n * (4 * SHIFTS + 4) + q_count * bins * 4,
            transcendentals=0,
        ),
    )(weighted, idx)


def shards(images, groups, references, interp_index, shell_index):
    n_cls = lax.axis_size("cls")
    n_vol = lax.axis_size("vol")
    n_half = lax.axis_size("half")
    part_count, pix_quarter = images.shape
    class_count = references.shape[0]
    capacity = max(2 * part_count // n_cls, 4)
    slot_count = n_cls * capacity
    owner_ids = groups[:, 0]
    matches = (owner_ids[:, None] == jnp.arange(n_cls, dtype=jnp.int32)[None, :]).astype(jnp.int32)
    order_in = jnp.sum(jnp.cumsum(matches, axis=0) * matches, axis=1) - 1
    slot_ids = owner_ids * capacity + order_in
    slot_hits = slot_ids[None, :] == jnp.arange(slot_count, dtype=jnp.int32)[:, None]
    outgoing = jnp.dot(
        slot_hits.astype(jnp.bfloat16), images, preferred_element_type=jnp.float32
    ).astype(jnp.bfloat16)
    arrived = lax.all_to_all(outgoing, "cls", split_axis=0, concat_axis=0, tiled=True)
    quarter_rows = pix_quarter // IMG
    bins = VOXS // IMG
    shaped_refs = references.reshape(class_count, quarter_rows, IMG)
    rolled_refs = jnp.concatenate(
        [
            jnp.roll(shaped_refs, -(shift_id - SHIFTS // 2), axis=2).reshape(
                class_count, pix_quarter
            )
            for shift_id in range(SHIFTS)
        ],
        axis=0,
    )
    partial_scores = lax.dot_general(
        arrived, rolled_refs, (((1,), (1,)), ((), ())), preferred_element_type=jnp.float32
    )
    partial_scores = partial_scores.reshape(slot_count, SHIFTS, class_count)
    scores = exchange_sum(partial_scores, "vol")
    squares = scores * scores
    mean_square = jnp.mean(squares, axis=(1, 2), keepdims=True)
    weights = (squares / (mean_square + EPS_W)).astype(jnp.bfloat16)
    weighted = lax.dot_general(
        weights.reshape(slot_count, SHIFTS * class_count),
        arrived,
        (((0,), (0,)), ((), ())),
        preferred_element_type=jnp.float32,
    )
    slab_part = project(
        weighted.reshape(SHIFTS, class_count * quarter_rows, IMG),
        interp_index.reshape(class_count * quarter_rows, IMG),
        bins,
    )
    piece_len = VOXS // (n_half * n_cls)
    slab_part = slab_part.reshape(n_half, n_cls, piece_len)
    own_block = reduce_scatter(slab_part, "cls").reshape(-1)
    half_id = lax.axis_index("half")
    other_block = partner(own_block, "half", 0)
    other_shell = partner(shell_index[0], "half", 0)
    first_block = jnp.where(half_id == 0, own_block, other_block)
    second_block = jnp.where(half_id == 0, other_block, own_block)
    shell_block = jnp.where(
        half_id == 0,
        jnp.concatenate([shell_index[0], other_shell]),
        jnp.concatenate([other_shell, shell_index[0]]),
    )
    block_hot = (shell_block[:, None] == jnp.arange(NSHELL, dtype=jnp.int32)[None, :]).astype(
        jnp.float32
    )
    stats = jnp.stack([first_block * first_block, second_block * second_block, first_block * second_block])
    shell_terms = jnp.dot(stats, block_hot, precision=lax.Precision.HIGHEST)
    shell_sums = exchange_sum(exchange_sum(shell_terms, "vol"), "cls")
    shell_fsc = shell_sums[2] / (jnp.sqrt(shell_sums[0]) * jnp.sqrt(shell_sums[1]) + EPS_F)
    mean_sq = (jnp.sum(shell_sums[0]) + jnp.sum(shell_sums[1]) + 2.0 * jnp.sum(shell_sums[2])) / (
        4.0 * n_vol * VOXS
    )
    first = lax.dynamic_index_in_dim(first_block.reshape(n_half, piece_len), half_id, keepdims=False)
    second = lax.dynamic_index_in_dim(second_block.reshape(n_half, piece_len), half_id, keepdims=False)
    shell_hot = (shell_index[0][:, None] == jnp.arange(NSHELL, dtype=jnp.int32)[None, :]).astype(
        jnp.float32
    )
    filter_vox = jnp.dot(shell_hot, shell_fsc, precision=lax.Precision.HIGHEST)
    volume = filter_vox * (0.5 * (first + second)) / jnp.sqrt(mean_sq + EPS_F)
    return (volume[None, :], shell_fsc)


def solution(mesh):
    placed = (
        P(("half", "cls"), "vol"),
        P(("half", "cls"), None),
        P("cls", "vol"),
        P("cls", "vol"),
        P("vol", ("half", "cls")),
    )
    return jax.shard_map(
        shards,
        mesh=mesh,
        in_specs=placed,
        out_specs=(P("vol", ("half", "cls")), P()),
        check_vma=False,
    )
```

```python
import functools

import jax
import jax.numpy as jnp
from jax import lax
from jax.experimental import pallas as pl
from jax.experimental.pallas import tpu as pltpu
from jax.sharding import PartitionSpec as P

IMG = 128
SHIFTS = 5
NSHELL = 128
PLANES = 4
VBOX = 256
VOXS = 262144


EPS_W = 1e-05
EPS_F = 1e-06

LO = 128
CLS = ("z", "x")
X_CHIPS = 4


def partner(shard, axis, apart):
    return lax.ppermute(shard, axis, [(i, i ^ 1 << apart) for i in range(lax.axis_size(axis))])


def digits_of(n):
    out, stride = [], 1
    while n % 4 == 0 and n > 1:
        out.append((stride, 4))
        stride, n = stride * 4, n // 4
    while n % 2 == 0 and n > 1:
        out.append((stride, 2))
        stride, n = stride * 2, n // 2
    return out


def shift_in_digit(x, axis, stride, radix, shift):
    n = lax.axis_size(axis)
    perm = []
    for i in range(n):
        d = (i // stride) % radix
        perm.append((i, i + ((d + shift) % radix - d) * stride))
    return lax.ppermute(x, axis, perm)


def butterfly_sum(x, axis):
    for bit in range(lax.axis_size(axis).bit_length() - 1):
        x = x + partner(x, axis, bit)
    return x


def exchange_sum(x, axis):
    n = lax.axis_size(axis)
    got = lax.all_to_all(jnp.broadcast_to(x[None], (n,) + x.shape), axis, 0, 0, tiled=True)
    total = got[0]
    for i in range(1, n):
        total = total + got[i]
    return total


def digit_sum(x, axis):
    me = lax.axis_index(axis)
    for stride, radix in digits_of(lax.axis_size(axis)):
        d = (me // stride) % radix
        got = jnp.stack([x] + [shift_in_digit(x, axis, stride, radix, s) for s in range(1, radix)])
        total = lax.dynamic_index_in_dim(got, d % radix, keepdims=False)
        for t in range(1, radix):
            total = total + lax.dynamic_index_in_dim(got, (d - t) % radix, keepdims=False)
        x = total
    return x


def reduce_scatter(x, inner, outer):
    me = lax.axis_index(inner)
    n_inner = lax.axis_size(inner)
    n_outer = lax.axis_size(outer)
    data = x
    for stride, radix in digits_of(n_inner):
        d = (me // stride) % radix
        data = data.reshape(data.shape[0], data.shape[1] // radix, radix, data.shape[2])
        total = lax.dynamic_index_in_dim(data, d, axis=2, keepdims=False)
        for s in range(1, radix):
            send = lax.dynamic_index_in_dim(data, (d + s) % radix, axis=2, keepdims=False)
            total = total + shift_in_digit(send, inner, stride, radix, s)
        data = total
    got = lax.all_to_all(jnp.swapaxes(data, 0, 1), outer, 0, 0, tiled=True)
    total = got[0]
    for i in range(1, n_outer):
        total = total + got[i]
    return total


def _project_kernel(w_ref, idx_ref, out_ref, wt_ref, it_ref):
    n = idx_ref.shape[0]
    hi_count = out_ref.shape[1]
    for shift_id in range(SHIFTS):
        wt_ref[shift_id] = w_ref[shift_id].T
    it_ref[...] = idx_ref[...].T
    lo_iota = lax.broadcasted_iota(jnp.int32, (LO, n), 0)
    hi_iota = lax.broadcasted_iota(jnp.int32, (hi_count, n), 0)

    def body(q, carry):
        v = wt_ref[0, pl.ds(lax.rem(q + SHIFTS // 2, IMG), 1), :]
        for shift_id in range(1, SHIFTS):
            row = lax.rem(q - (shift_id - SHIFTS // 2) + IMG, IMG)
            v = v + wt_ref[shift_id, pl.ds(row, 1), :]
        idx = it_ref[pl.ds(q, 1), :]
        lo = jnp.bitwise_and(idx, LO - 1)
        hi = jnp.right_shift(idx, 7)
        rt = jnp.where(lo == lo_iota, 1.0, 0.0).astype(jnp.bfloat16)
        vh = v.astype(jnp.bfloat16)
        vl = (v - vh.astype(jnp.float32)).astype(jnp.bfloat16)
        mask = hi == hi_iota
        zero = jnp.zeros((), jnp.bfloat16)
        lt = jnp.concatenate([jnp.where(mask, vh, zero), jnp.where(mask, vl, zero)], axis=0)
        o = lax.dot_general(lt, rt, (((1,), (1,)), ((), ())), preferred_element_type=jnp.float32)
        out_ref[q] = o[:hi_count] + o[hi_count:]
        return carry

    lax.fori_loop(0, IMG, body, 0, unroll=16)


def project(weighted, idx, bins):
    n, q_count = idx.shape
    hi_count = bins // LO
    return pl.pallas_call(
        _project_kernel,
        out_shape=jax.ShapeDtypeStruct((q_count, hi_count, LO), jnp.float32),
        in_specs=[
            pl.BlockSpec(memory_space=pltpu.VMEM),
            pl.BlockSpec(memory_space=pltpu.VMEM),
        ],
        out_specs=pl.BlockSpec(memory_space=pltpu.VMEM),
        scratch_shapes=[
            pltpu.VMEM((SHIFTS, q_count, n), jnp.float32),
            pltpu.VMEM((q_count, n), jnp.int32),
        ],
        cost_estimate=pl.CostEstimate(
            flops=2 * q_count * 2 * hi_count * LO * n,
            bytes_accessed=q_count * n * (4 * SHIFTS + 4) + q_count * bins * 4,
            transcendentals=0,
        ),
    )(weighted, idx)


def shards(images, groups, references, interp_index, shell_index):
    n_cls = lax.axis_size(CLS)
    n_vol = lax.axis_size("vol")
    n_half = lax.axis_size("half")
    part_count, pix_quarter = images.shape
    class_count = references.shape[0]
    capacity = max(2 * part_count // n_cls, 4)
    slot_count = n_cls * capacity
    owner_ids = groups[:, 0]
    matches = (owner_ids[:, None] == jnp.arange(n_cls, dtype=jnp.int32)[None, :]).astype(jnp.int32)
    order_in = jnp.sum(jnp.cumsum(matches, axis=0) * matches, axis=1) - 1
    slot_ids = owner_ids * capacity + order_in
    slot_hits = slot_ids[None, :] == jnp.arange(slot_count, dtype=jnp.int32)[:, None]
    outgoing = jnp.dot(
        slot_hits.astype(jnp.bfloat16), images, preferred_element_type=jnp.float32
    ).astype(jnp.bfloat16)
    arrived = lax.all_to_all(outgoing, CLS, split_axis=0, concat_axis=0, tiled=True)
    quarter_rows = pix_quarter // IMG
    bins = VOXS // IMG
    shaped_refs = references.reshape(class_count, quarter_rows, IMG)
    rolled_refs = jnp.concatenate(
        [
            jnp.roll(shaped_refs, -(shift_id - SHIFTS // 2), axis=2).reshape(
                class_count, pix_quarter
            )
            for shift_id in range(SHIFTS)
        ],
        axis=0,
    )
    partial_scores = lax.dot_general(
        arrived, rolled_refs, (((1,), (1,)), ((), ())), preferred_element_type=jnp.float32
    )
    partial_scores = partial_scores.reshape(slot_count, SHIFTS, class_count)
    scores = exchange_sum(partial_scores, "vol")
    squares = scores * scores
    mean_square = jnp.mean(squares, axis=(1, 2), keepdims=True)
    weights = (squares / (mean_square + EPS_W)).astype(jnp.bfloat16)
    weighted = lax.dot_general(
        weights.reshape(slot_count, SHIFTS * class_count),
        arrived,
        (((0,), (0,)), ((), ())),
        preferred_element_type=jnp.float32,
    )
    slab_part = project(
        weighted.reshape(SHIFTS, class_count * quarter_rows, IMG),
        interp_index.reshape(class_count * quarter_rows, IMG),
        bins,
    )
    piece_len = VOXS // (n_half * n_cls)
    slab_part = slab_part.reshape(n_half, n_cls, piece_len)
    own_block = reduce_scatter(slab_part, "x", "z").reshape(-1)
    half_id = lax.axis_index("half")
    other_block = partner(own_block, "half", 0)
    other_shell = partner(shell_index[0], "half", 0)
    first_block = jnp.where(half_id == 0, own_block, other_block)
    second_block = jnp.where(half_id == 0, other_block, own_block)
    shell_block = jnp.where(
        half_id == 0,
        jnp.concatenate([shell_index[0], other_shell]),
        jnp.concatenate([other_shell, shell_index[0]]),
    )
    block_hot = (shell_block[:, None] == jnp.arange(NSHELL, dtype=jnp.int32)[None, :]).astype(
        jnp.float32
    )
    stats = jnp.stack([first_block * first_block, second_block * second_block, first_block * second_block])
    shell_terms = jnp.dot(stats, block_hot, precision=lax.Precision.HIGHEST)
    shell_sums = exchange_sum(exchange_sum(shell_terms, "vol"), CLS)
    shell_fsc = shell_sums[2] / (jnp.sqrt(shell_sums[0]) * jnp.sqrt(shell_sums[1]) + EPS_F)
    mean_sq = (jnp.sum(shell_sums[0]) + jnp.sum(shell_sums[1]) + 2.0 * jnp.sum(shell_sums[2])) / (
        4.0 * n_vol * VOXS
    )
    first = lax.dynamic_index_in_dim(first_block.reshape(n_half, piece_len), half_id, keepdims=False)
    second = lax.dynamic_index_in_dim(second_block.reshape(n_half, piece_len), half_id, keepdims=False)
    shell_hot = (shell_index[0][:, None] == jnp.arange(NSHELL, dtype=jnp.int32)[None, :]).astype(
        jnp.float32
    )
    filter_vox = jnp.dot(shell_hot, shell_fsc, precision=lax.Precision.HIGHEST)
    volume = filter_vox * (0.5 * (first + second)) / jnp.sqrt(mean_sq + EPS_F)
    return (volume[None, :], shell_fsc)


def solution(mesh):
    n_cls = mesh.shape["cls"]
    fine = jax.sharding.Mesh(
        mesh.devices.reshape(mesh.shape["half"], n_cls // X_CHIPS, X_CHIPS, mesh.shape["vol"]),
        ("half", "z", "x", "vol"),
    )
    rows = ("half", "z", "x")
    placed = (
        P(rows, "vol"),
        P(rows, None),
        P(CLS, "vol"),
        P(CLS, "vol"),
        P("vol", rows),
    )
    return jax.shard_map(
        shards,
        mesh=fine,
        in_specs=placed,
        out_specs=(P("vol", rows), P()),
        check_vma=False,
    )
```

```python
import functools

import jax
import jax.numpy as jnp
from jax import lax
from jax.experimental import pallas as pl
from jax.experimental.pallas import tpu as pltpu
from jax.sharding import PartitionSpec as P

IMG = 128
SHIFTS = 5
NSHELL = 128
PLANES = 4
VBOX = 256
VOXS = 262144


EPS_W = 1e-05
EPS_F = 1e-06

LO = 128
CLS = ("z", "x")
X_CHIPS = 4


def partner(shard, axis, apart):
    return lax.ppermute(shard, axis, [(i, i ^ 1 << apart) for i in range(lax.axis_size(axis))])


def digits_of(n):
    out, stride = [], 1
    while n % 4 == 0 and n > 1:
        out.append((stride, 4))
        stride, n = stride * 4, n // 4
    while n % 2 == 0 and n > 1:
        out.append((stride, 2))
        stride, n = stride * 2, n // 2
    return out


def shift_in_digit(x, axis, stride, radix, shift):
    n = lax.axis_size(axis)
    perm = []
    for i in range(n):
        d = (i // stride) % radix
        perm.append((i, i + ((d + shift) % radix - d) * stride))
    return lax.ppermute(x, axis, perm)


def butterfly_sum(x, axis):
    for bit in range(lax.axis_size(axis).bit_length() - 1):
        x = x + partner(x, axis, bit)
    return x


def exchange_sum(x, axis):
    n = lax.axis_size(axis)
    got = lax.all_to_all(jnp.broadcast_to(x[None], (n,) + x.shape), axis, 0, 0, tiled=True)
    total = got[0]
    for i in range(1, n):
        total = total + got[i]
    return total


def digit_sum(x, axis):
    me = lax.axis_index(axis)
    for stride, radix in digits_of(lax.axis_size(axis)):
        d = (me // stride) % radix
        got = jnp.stack([x] + [shift_in_digit(x, axis, stride, radix, s) for s in range(1, radix)])
        total = lax.dynamic_index_in_dim(got, d % radix, keepdims=False)
        for t in range(1, radix):
            total = total + lax.dynamic_index_in_dim(got, (d - t) % radix, keepdims=False)
        x = total
    return x


def exchange_rows(data, axis):
    n = lax.axis_size(axis)
    got = lax.all_to_all(jnp.moveaxis(data, 1, 0), axis, 0, 0, tiled=True)
    total = got[0]
    for i in range(1, n):
        total = total + got[i]
    return total


def reduce_scatter(x, inner, outer):
    n_inner = lax.axis_size(inner)
    n_outer = lax.axis_size(outer)
    a, _, length = x.shape
    data = exchange_rows(jnp.swapaxes(x.reshape(a, n_outer, n_inner, length), 1, 2), inner)
    return exchange_rows(data.reshape(a, n_outer, 1, length), outer)[:, 0]


def _project_kernel(w_ref, idx_ref, out_ref, wt_ref, it_ref):
    n = idx_ref.shape[0]
    hi_count = out_ref.shape[1]
    for shift_id in range(SHIFTS):
        wt_ref[shift_id] = w_ref[shift_id].T
    it_ref[...] = idx_ref[...].T
    lo_iota = lax.broadcasted_iota(jnp.int32, (LO, n), 0)
    hi_iota = lax.broadcasted_iota(jnp.int32, (hi_count, n), 0)

    def body(q, carry):
        v = wt_ref[0, pl.ds(lax.rem(q + SHIFTS // 2, IMG), 1), :]
        for shift_id in range(1, SHIFTS):
            row = lax.rem(q - (shift_id - SHIFTS // 2) + IMG, IMG)
            v = v + wt_ref[shift_id, pl.ds(row, 1), :]
        idx = it_ref[pl.ds(q, 1), :]
        lo = jnp.bitwise_and(idx, LO - 1)
        hi = jnp.right_shift(idx, 7)
        rt = jnp.where(lo == lo_iota, 1.0, 0.0).astype(jnp.bfloat16)
        vh = v.astype(jnp.bfloat16)
        vl = (v - vh.astype(jnp.float32)).astype(jnp.bfloat16)
        mask = hi == hi_iota
        zero = jnp.zeros((), jnp.bfloat16)
        lt = jnp.concatenate([jnp.where(mask, vh, zero), jnp.where(mask, vl, zero)], axis=0)
        o = lax.dot_general(lt, rt, (((1,), (1,)), ((), ())), preferred_element_type=jnp.float32)
        out_ref[q] = o[:hi_count] + o[hi_count:]
        return carry

    lax.fori_loop(0, IMG, body, 0, unroll=16)


def project(weighted, idx, bins):
    n, q_count = idx.shape
    hi_count = bins // LO
    return pl.pallas_call(
        _project_kernel,
        out_shape=jax.ShapeDtypeStruct((q_count, hi_count, LO), jnp.float32),
        in_specs=[
            pl.BlockSpec(memory_space=pltpu.VMEM),
            pl.BlockSpec(memory_space=pltpu.VMEM),
        ],
        out_specs=pl.BlockSpec(memory_space=pltpu.VMEM),
        scratch_shapes=[
            pltpu.VMEM((SHIFTS, q_count, n), jnp.float32),
            pltpu.VMEM((q_count, n), jnp.int32),
        ],
        cost_estimate=pl.CostEstimate(
            flops=2 * q_count * 2 * hi_count * LO * n,
            bytes_accessed=q_count * n * (4 * SHIFTS + 4) + q_count * bins * 4,
            transcendentals=0,
        ),
    )(weighted, idx)


def shards(images, groups, references, interp_index, shell_index):
    n_cls = lax.axis_size(CLS)
    n_vol = lax.axis_size("vol")
    n_half = lax.axis_size("half")
    part_count, pix_quarter = images.shape
    class_count = references.shape[0]
    capacity = max(2 * part_count // n_cls, 4)
    slot_count = n_cls * capacity
    owner_ids = groups[:, 0]
    matches = (owner_ids[:, None] == jnp.arange(n_cls, dtype=jnp.int32)[None, :]).astype(jnp.int32)
    order_in = jnp.sum(jnp.cumsum(matches, axis=0) * matches, axis=1) - 1
    slot_ids = owner_ids * capacity + order_in
    slot_hits = slot_ids[None, :] == jnp.arange(slot_count, dtype=jnp.int32)[:, None]
    outgoing = jnp.dot(
        slot_hits.astype(jnp.bfloat16), images, preferred_element_type=jnp.float32
    ).astype(jnp.bfloat16)
    arrived = lax.all_to_all(outgoing, CLS, split_axis=0, concat_axis=0, tiled=True)
    quarter_rows = pix_quarter // IMG
    bins = VOXS // IMG
    shaped_refs = references.reshape(class_count, quarter_rows, IMG)
    rolled_refs = jnp.concatenate(
        [
            jnp.roll(shaped_refs, -(shift_id - SHIFTS // 2), axis=2).reshape(
                class_count, pix_quarter
            )
            for shift_id in range(SHIFTS)
        ],
        axis=0,
    )
    partial_scores = lax.dot_general(
        arrived, rolled_refs, (((1,), (1,)), ((), ())), preferred_element_type=jnp.float32
    )
    partial_scores = partial_scores.reshape(slot_count, SHIFTS, class_count)
    scores = exchange_sum(partial_scores, "vol")
    squares = scores * scores
    mean_square = jnp.mean(squares, axis=(1, 2), keepdims=True)
    weights = (squares / (mean_square + EPS_W)).astype(jnp.bfloat16)
    weighted = lax.dot_general(
        weights,
        arrived.reshape(slot_count, quarter_rows, IMG),
        (((0,), (0,)), ((), ())),
        preferred_element_type=jnp.float32,
    )
    slab_part = project(
        weighted.reshape(SHIFTS, class_count * quarter_rows, IMG),
        interp_index.reshape(class_count * quarter_rows, IMG),
        bins,
    )
    piece_len = VOXS // (n_half * n_cls)
    slab_part = slab_part.reshape(n_half, n_cls, piece_len)
    own_block = reduce_scatter(slab_part, "x", "z").reshape(-1)
    half_id = lax.axis_index("half")
    other_block = partner(own_block, "half", 0)
    other_shell = partner(shell_index[0], "half", 0)
    first_block = jnp.where(half_id == 0, own_block, other_block)
    second_block = jnp.where(half_id == 0, other_block, own_block)
    shell_block = jnp.where(
        half_id == 0,
        jnp.concatenate([shell_index[0], other_shell]),
        jnp.concatenate([other_shell, shell_index[0]]),
    )
    block_hot = (shell_block[:, None] == jnp.arange(NSHELL, dtype=jnp.int32)[None, :]).astype(
        jnp.float32
    )
    stats = jnp.stack([first_block * first_block, second_block * second_block, first_block * second_block])
    shell_terms = jnp.dot(stats, block_hot, precision=lax.Precision.HIGHEST)
    shell_sums = exchange_sum(exchange_sum(shell_terms, "vol"), CLS)
    shell_fsc = shell_sums[2] / (jnp.sqrt(shell_sums[0]) * jnp.sqrt(shell_sums[1]) + EPS_F)
    mean_sq = (jnp.sum(shell_sums[0]) + jnp.sum(shell_sums[1]) + 2.0 * jnp.sum(shell_sums[2])) / (
        4.0 * n_vol * VOXS
    )
    first = lax.dynamic_index_in_dim(first_block.reshape(n_half, piece_len), half_id, keepdims=False)
    second = lax.dynamic_index_in_dim(second_block.reshape(n_half, piece_len), half_id, keepdims=False)
    shell_hot = (shell_index[0][:, None] == jnp.arange(NSHELL, dtype=jnp.int32)[None, :]).astype(
        jnp.float32
    )
    filter_vox = jnp.dot(shell_hot, shell_fsc, precision=lax.Precision.HIGHEST)
    volume = filter_vox * (0.5 * (first + second)) / jnp.sqrt(mean_sq + EPS_F)
    return (volume[None, :], shell_fsc)


def solution(mesh):
    n_cls = mesh.shape["cls"]
    fine = jax.sharding.Mesh(
        mesh.devices.reshape(mesh.shape["half"], n_cls // X_CHIPS, X_CHIPS, mesh.shape["vol"]),
        ("half", "z", "x", "vol"),
    )
    rows = ("half", "z", "x")
    placed = (
        P(rows, "vol"),
        P(rows, None),
        P(CLS, "vol"),
        P(CLS, "vol"),
        P("vol", rows),
    )
    return jax.shard_map(
        shards,
        mesh=fine,
        in_specs=placed,
        out_specs=(P("vol", rows), P()),
        check_vma=False,
    )
```

```python
import functools

import jax
import jax.numpy as jnp
from jax import lax
from jax.experimental import pallas as pl
from jax.experimental.pallas import tpu as pltpu
from jax.sharding import PartitionSpec as P

IMG = 128
SHIFTS = 5
NSHELL = 128
PLANES = 4
VBOX = 256
VOXS = 262144


EPS_W = 1e-05
EPS_F = 1e-06

LO = 128
CLS = ("z", "x")
X_CHIPS = 4


def partner(shard, axis, apart):
    return lax.ppermute(shard, axis, [(i, i ^ 1 << apart) for i in range(lax.axis_size(axis))])


def digits_of(n):
    out, stride = [], 1
    while n % 4 == 0 and n > 1:
        out.append((stride, 4))
        stride, n = stride * 4, n // 4
    while n % 2 == 0 and n > 1:
        out.append((stride, 2))
        stride, n = stride * 2, n // 2
    return out


def shift_in_digit(x, axis, stride, radix, shift):
    n = lax.axis_size(axis)
    perm = []
    for i in range(n):
        d = (i // stride) % radix
        perm.append((i, i + ((d + shift) % radix - d) * stride))
    return lax.ppermute(x, axis, perm)


def butterfly_sum(x, axis):
    for bit in range(lax.axis_size(axis).bit_length() - 1):
        x = x + partner(x, axis, bit)
    return x


def exchange_sum(x, axis):
    n = lax.axis_size(axis)
    got = lax.all_to_all(jnp.broadcast_to(x[None], (n,) + x.shape), axis, 0, 0, tiled=True)
    total = got[0]
    for i in range(1, n):
        total = total + got[i]
    return total


def digit_sum(x, axis):
    me = lax.axis_index(axis)
    for stride, radix in digits_of(lax.axis_size(axis)):
        d = (me // stride) % radix
        got = jnp.stack([x] + [shift_in_digit(x, axis, stride, radix, s) for s in range(1, radix)])
        total = lax.dynamic_index_in_dim(got, d % radix, keepdims=False)
        for t in range(1, radix):
            total = total + lax.dynamic_index_in_dim(got, (d - t) % radix, keepdims=False)
        x = total
    return x


def exchange_rows(data, axis):
    n = lax.axis_size(axis)
    got = lax.all_to_all(jnp.moveaxis(data, 1, 0), axis, 0, 0, tiled=True)
    total = got[0]
    for i in range(1, n):
        total = total + got[i]
    return total


def reduce_scatter(x, inner, outer):
    n_inner = lax.axis_size(inner)
    n_outer = lax.axis_size(outer)
    a, _, length = x.shape
    data = exchange_rows(jnp.swapaxes(x.reshape(a, n_outer, n_inner, length), 1, 2), inner)
    return exchange_rows(data.reshape(a, n_outer, 1, length), outer)[:, 0]


def _project_kernel(w_ref, idx_ref, out_ref, wt_ref, it_ref):
    n = idx_ref.shape[0]
    hi_count = out_ref.shape[1]
    for shift_id in range(SHIFTS):
        wt_ref[shift_id] = w_ref[shift_id].T
    it_ref[...] = idx_ref[...].T
    lo_iota = lax.broadcasted_iota(jnp.int32, (LO, n), 0)
    hi_iota = lax.broadcasted_iota(jnp.int32, (hi_count, n), 0)

    def body(q, carry):
        v = wt_ref[0, pl.ds(lax.rem(q + SHIFTS // 2, IMG), 1), :]
        for shift_id in range(1, SHIFTS):
            row = lax.rem(q - (shift_id - SHIFTS // 2) + IMG, IMG)
            v = v + wt_ref[shift_id, pl.ds(row, 1), :]
        idx = it_ref[pl.ds(q, 1), :]
        lo = jnp.bitwise_and(idx, LO - 1)
        hi = jnp.right_shift(idx, 7)
        rt = jnp.where(lo == lo_iota, 1.0, 0.0).astype(jnp.bfloat16)
        vh = v.astype(jnp.bfloat16)
        vl = (v - vh.astype(jnp.float32)).astype(jnp.bfloat16)
        mask = hi == hi_iota
        zero = jnp.zeros((), jnp.bfloat16)
        lt = jnp.concatenate([jnp.where(mask, vh, zero), jnp.where(mask, vl, zero)], axis=0)
        o = lax.dot_general(lt, rt, (((1,), (1,)), ((), ())), preferred_element_type=jnp.float32)
        out_ref[q] = o[:hi_count] + o[hi_count:]
        return carry

    lax.fori_loop(0, IMG, body, 0, unroll=16)


def project(weighted, idx, bins):
    n, q_count = idx.shape
    hi_count = bins // LO
    return pl.pallas_call(
        _project_kernel,
        out_shape=jax.ShapeDtypeStruct((q_count, hi_count, LO), jnp.float32),
        in_specs=[
            pl.BlockSpec(memory_space=pltpu.VMEM),
            pl.BlockSpec(memory_space=pltpu.VMEM),
        ],
        out_specs=pl.BlockSpec(memory_space=pltpu.VMEM),
        scratch_shapes=[
            pltpu.VMEM((SHIFTS, q_count, n), jnp.float32),
            pltpu.VMEM((q_count, n), jnp.int32),
        ],
        cost_estimate=pl.CostEstimate(
            flops=2 * q_count * 2 * hi_count * LO * n,
            bytes_accessed=q_count * n * (4 * SHIFTS + 4) + q_count * bins * 4,
            transcendentals=0,
        ),
    )(weighted, idx)


def shards(images, groups, references, interp_index, shell_index):
    n_cls = lax.axis_size(CLS)
    n_vol = lax.axis_size("vol")
    n_half = lax.axis_size("half")
    part_count, pix_quarter = images.shape
    class_count = references.shape[0]
    capacity = max(2 * part_count // n_cls, 4)
    slot_count = n_cls * capacity
    owner_ids = groups[:, 0]
    matches = (owner_ids[:, None] == jnp.arange(n_cls, dtype=jnp.int32)[None, :]).astype(jnp.int32)
    order_in = jnp.sum(jnp.cumsum(matches, axis=0) * matches, axis=1) - 1
    slot_ids = owner_ids * capacity + order_in
    slot_hits = slot_ids[None, :] == jnp.arange(slot_count, dtype=jnp.int32)[:, None]
    quarter_rows = pix_quarter // IMG
    bins = VOXS // IMG
    outgoing = lax.dot_general(
        slot_hits.astype(jnp.bfloat16),
        images.reshape(part_count, quarter_rows, IMG),
        (((1,), (0,)), ((), ())),
        preferred_element_type=jnp.float32,
    ).astype(jnp.bfloat16)
    arrived = lax.all_to_all(
        outgoing.reshape(n_cls, capacity, quarter_rows, IMG), CLS, split_axis=0, concat_axis=0, tiled=True
    ).reshape(slot_count, quarter_rows, IMG)
    shaped_refs = references.reshape(class_count, quarter_rows, IMG)
    rolled_refs = jnp.concatenate(
        [jnp.roll(shaped_refs, -(shift_id - SHIFTS // 2), axis=2) for shift_id in range(SHIFTS)],
        axis=0,
    )
    partial_scores = lax.dot_general(
        arrived, rolled_refs, (((1, 2), (1, 2)), ((), ())), preferred_element_type=jnp.float32
    )
    partial_scores = partial_scores.reshape(slot_count, SHIFTS, class_count)
    scores = exchange_sum(partial_scores, "vol")
    squares = scores * scores
    mean_square = jnp.mean(squares, axis=(1, 2), keepdims=True)
    weights = (squares / (mean_square + EPS_W)).astype(jnp.bfloat16)
    weighted = lax.dot_general(
        weights.reshape(slot_count, SHIFTS * class_count),
        arrived,
        (((0,), (0,)), ((), ())),
        preferred_element_type=jnp.float32,
    )
    slab_part = project(
        weighted.reshape(SHIFTS, class_count * quarter_rows, IMG),
        interp_index.reshape(class_count * quarter_rows, IMG),
        bins,
    )
    piece_len = VOXS // (n_half * n_cls)
    slab_part = slab_part.reshape(n_half, n_cls, piece_len)
    own_block = reduce_scatter(slab_part, "x", "z").reshape(-1)
    half_id = lax.axis_index("half")
    other_block = partner(own_block, "half", 0)
    other_shell = partner(shell_index[0], "half", 0)
    first_block = jnp.where(half_id == 0, own_block, other_block)
    second_block = jnp.where(half_id == 0, other_block, own_block)
    shell_block = jnp.where(
        half_id == 0,
        jnp.concatenate([shell_index[0], other_shell]),
        jnp.concatenate([other_shell, shell_index[0]]),
    )
    block_hot = (shell_block[:, None] == jnp.arange(NSHELL, dtype=jnp.int32)[None, :]).astype(
        jnp.float32
    )
    stats = jnp.stack([first_block * first_block, second_block * second_block, first_block * second_block])
    shell_terms = jnp.dot(stats, block_hot, precision=lax.Precision.HIGHEST)
    shell_sums = exchange_sum(exchange_sum(shell_terms, "vol"), CLS)
    shell_fsc = shell_sums[2] / (jnp.sqrt(shell_sums[0]) * jnp.sqrt(shell_sums[1]) + EPS_F)
    mean_sq = (jnp.sum(shell_sums[0]) + jnp.sum(shell_sums[1]) + 2.0 * jnp.sum(shell_sums[2])) / (
        4.0 * n_vol * VOXS
    )
    first = lax.dynamic_index_in_dim(first_block.reshape(n_half, piece_len), half_id, keepdims=False)
    second = lax.dynamic_index_in_dim(second_block.reshape(n_half, piece_len), half_id, keepdims=False)
    shell_hot = (shell_index[0][:, None] == jnp.arange(NSHELL, dtype=jnp.int32)[None, :]).astype(
        jnp.float32
    )
    filter_vox = jnp.dot(shell_hot, shell_fsc, precision=lax.Precision.HIGHEST)
    volume = filter_vox * (0.5 * (first + second)) / jnp.sqrt(mean_sq + EPS_F)
    return (volume[None, :], shell_fsc)


def solution(mesh):
    n_cls = mesh.shape["cls"]
    fine = jax.sharding.Mesh(
        mesh.devices.reshape(mesh.shape["half"], n_cls // X_CHIPS, X_CHIPS, mesh.shape["vol"]),
        ("half", "z", "x", "vol"),
    )
    rows = ("half", "z", "x")
    placed = (
        P(rows, "vol"),
        P(rows, None),
        P(CLS, "vol"),
        P(CLS, "vol"),
        P("vol", rows),
    )
    return jax.shard_map(
        shards,
        mesh=fine,
        in_specs=placed,
        out_specs=(P("vol", rows), P()),
        check_vma=False,
    )
```

```python
import functools

import jax
import jax.numpy as jnp
from jax import lax
from jax.experimental import pallas as pl
from jax.experimental.pallas import tpu as pltpu
from jax.sharding import PartitionSpec as P

IMG = 128
SHIFTS = 5
NSHELL = 128
PLANES = 4
VBOX = 256
VOXS = 262144


EPS_W = 1e-05
EPS_F = 1e-06

LO = 128
CLS = ("z", "x")
X_CHIPS = 4


def partner(shard, axis, apart):
    return lax.ppermute(shard, axis, [(i, i ^ 1 << apart) for i in range(lax.axis_size(axis))])


def digits_of(n):
    out, stride = [], 1
    while n % 4 == 0 and n > 1:
        out.append((stride, 4))
        stride, n = stride * 4, n // 4
    while n % 2 == 0 and n > 1:
        out.append((stride, 2))
        stride, n = stride * 2, n // 2
    return out


def shift_in_digit(x, axis, stride, radix, shift):
    n = lax.axis_size(axis)
    perm = []
    for i in range(n):
        d = (i // stride) % radix
        perm.append((i, i + ((d + shift) % radix - d) * stride))
    return lax.ppermute(x, axis, perm)


def butterfly_sum(x, axis):
    for bit in range(lax.axis_size(axis).bit_length() - 1):
        x = x + partner(x, axis, bit)
    return x


def exchange_sum(x, axis):
    n = lax.axis_size(axis)
    got = lax.all_to_all(jnp.broadcast_to(x[None], (n,) + x.shape), axis, 0, 0, tiled=True)
    total = got[0]
    for i in range(1, n):
        total = total + got[i]
    return total


def digit_sum(x, axis):
    me = lax.axis_index(axis)
    for stride, radix in digits_of(lax.axis_size(axis)):
        d = (me // stride) % radix
        got = jnp.stack([x] + [shift_in_digit(x, axis, stride, radix, s) for s in range(1, radix)])
        total = lax.dynamic_index_in_dim(got, d % radix, keepdims=False)
        for t in range(1, radix):
            total = total + lax.dynamic_index_in_dim(got, (d - t) % radix, keepdims=False)
        x = total
    return x


def exchange_rows(data, axis):
    n = lax.axis_size(axis)
    got = lax.all_to_all(jnp.moveaxis(data, 1, 0), axis, 0, 0, tiled=True)
    total = got[0]
    for i in range(1, n):
        total = total + got[i]
    return total


def reduce_scatter(x, inner, outer):
    n_half = lax.axis_size("half")
    n_inner = lax.axis_size(inner)
    n_outer = lax.axis_size(outer)
    length = x.shape[2]
    data = x.reshape(n_half, n_outer, n_inner, length).transpose(0, 2, 1, 3)
    got = lax.all_to_all(
        data.reshape(n_half * n_inner, n_outer, length), ("half", inner), 0, 0, tiled=True
    ).reshape(n_half, n_inner, n_outer, length)
    part = got[:, 0]
    for i in range(1, n_inner):
        part = part + got[:, i]
    got = lax.all_to_all(jnp.swapaxes(part, 0, 1), outer, 0, 0, tiled=True)
    total = got[0]
    for i in range(1, n_outer):
        total = total + got[i]
    return total


def _project_kernel(w_ref, idx_ref, out_ref, wt_ref, it_ref):
    n = idx_ref.shape[0]
    hi_count = out_ref.shape[1]
    for shift_id in range(SHIFTS):
        wt_ref[shift_id] = w_ref[shift_id].T
    it_ref[...] = idx_ref[...].T
    lo_iota = lax.broadcasted_iota(jnp.int32, (LO, n), 0)
    hi_iota = lax.broadcasted_iota(jnp.int32, (hi_count, n), 0)

    def body(q, carry):
        v = wt_ref[0, pl.ds(lax.rem(q + SHIFTS // 2, IMG), 1), :]
        for shift_id in range(1, SHIFTS):
            row = lax.rem(q - (shift_id - SHIFTS // 2) + IMG, IMG)
            v = v + wt_ref[shift_id, pl.ds(row, 1), :]
        idx = it_ref[pl.ds(q, 1), :]
        lo = jnp.bitwise_and(idx, LO - 1)
        hi = jnp.right_shift(idx, 7)
        rt = jnp.where(lo == lo_iota, 1.0, 0.0).astype(jnp.bfloat16)
        vh = v.astype(jnp.bfloat16)
        vl = (v - vh.astype(jnp.float32)).astype(jnp.bfloat16)
        mask = hi == hi_iota
        zero = jnp.zeros((), jnp.bfloat16)
        lt = jnp.concatenate([jnp.where(mask, vh, zero), jnp.where(mask, vl, zero)], axis=0)
        o = lax.dot_general(lt, rt, (((1,), (1,)), ((), ())), preferred_element_type=jnp.float32)
        out_ref[q] = o[:hi_count] + o[hi_count:]
        return carry

    lax.fori_loop(0, IMG, body, 0, unroll=16)


def project(weighted, idx, bins):
    n, q_count = idx.shape
    hi_count = bins // LO
    return pl.pallas_call(
        _project_kernel,
        out_shape=jax.ShapeDtypeStruct((q_count, hi_count, LO), jnp.float32),
        in_specs=[
            pl.BlockSpec(memory_space=pltpu.VMEM),
            pl.BlockSpec(memory_space=pltpu.VMEM),
        ],
        out_specs=pl.BlockSpec(memory_space=pltpu.VMEM),
        scratch_shapes=[
            pltpu.VMEM((SHIFTS, q_count, n), jnp.float32),
            pltpu.VMEM((q_count, n), jnp.int32),
        ],
        cost_estimate=pl.CostEstimate(
            flops=2 * q_count * 2 * hi_count * LO * n,
            bytes_accessed=q_count * n * (4 * SHIFTS + 4) + q_count * bins * 4,
            transcendentals=0,
        ),
    )(weighted, idx)


def shards(images, groups, references, interp_index, shell_index):
    n_cls = lax.axis_size(CLS)
    n_vol = lax.axis_size("vol")
    n_half = lax.axis_size("half")
    part_count, pix_quarter = images.shape
    class_count = references.shape[0]
    capacity = max(2 * part_count // n_cls, 4)
    slot_count = n_cls * capacity
    owner_ids = groups[:, 0]
    matches = (owner_ids[:, None] == jnp.arange(n_cls, dtype=jnp.int32)[None, :]).astype(jnp.int32)
    order_in = jnp.sum(jnp.cumsum(matches, axis=0) * matches, axis=1) - 1
    slot_ids = owner_ids * capacity + order_in
    slot_hits = slot_ids[None, :] == jnp.arange(slot_count, dtype=jnp.int32)[:, None]
    quarter_rows = pix_quarter // IMG
    bins = VOXS // IMG
    outgoing = lax.dot_general(
        slot_hits.astype(jnp.bfloat16),
        images.reshape(part_count, quarter_rows, IMG),
        (((1,), (0,)), ((), ())),
        preferred_element_type=jnp.float32,
    ).astype(jnp.bfloat16)
    arrived = lax.all_to_all(
        outgoing.reshape(n_cls, capacity, quarter_rows, IMG), CLS, split_axis=0, concat_axis=0, tiled=True
    ).reshape(slot_count, quarter_rows, IMG)
    shaped_refs = references.reshape(class_count, quarter_rows, IMG)
    rolled_refs = jnp.concatenate(
        [jnp.roll(shaped_refs, -(shift_id - SHIFTS // 2), axis=2) for shift_id in range(SHIFTS)],
        axis=0,
    )
    partial_scores = lax.dot_general(
        arrived, rolled_refs, (((1, 2), (1, 2)), ((), ())), preferred_element_type=jnp.float32
    )
    partial_scores = partial_scores.reshape(slot_count, SHIFTS, class_count)
    scores = exchange_sum(partial_scores, "vol")
    squares = scores * scores
    mean_square = jnp.mean(squares, axis=(1, 2), keepdims=True)
    weights = (squares / (mean_square + EPS_W)).astype(jnp.bfloat16)
    weighted = lax.dot_general(
        weights.reshape(slot_count, SHIFTS * class_count),
        arrived,
        (((0,), (0,)), ((), ())),
        preferred_element_type=jnp.float32,
    )
    slab_part = project(
        weighted.reshape(SHIFTS, class_count * quarter_rows, IMG),
        interp_index.reshape(class_count * quarter_rows, IMG),
        bins,
    )
    piece_len = VOXS // (n_half * n_cls)
    slab_part = slab_part.reshape(n_half, n_cls, piece_len)
    maps = reduce_scatter(slab_part, "x", "z")
    first = maps[0]
    second = maps[1]
    shell_hot = (shell_index[0][:, None] == jnp.arange(NSHELL, dtype=jnp.int32)[None, :]).astype(
        jnp.float32
    )
    stats = jnp.stack([first * first, second * second, first * second])
    shell_terms = jnp.dot(stats, shell_hot, precision=lax.Precision.HIGHEST)
    shell_sums = exchange_sum(exchange_sum(shell_terms, ("half", "vol")), CLS)
    shell_fsc = shell_sums[2] / (jnp.sqrt(shell_sums[0]) * jnp.sqrt(shell_sums[1]) + EPS_F)
    mean_sq = (jnp.sum(shell_sums[0]) + jnp.sum(shell_sums[1]) + 2.0 * jnp.sum(shell_sums[2])) / (
        4.0 * n_vol * VOXS
    )
    filter_vox = jnp.dot(shell_hot, shell_fsc, precision=lax.Precision.HIGHEST)
    volume = filter_vox * (0.5 * (first + second)) / jnp.sqrt(mean_sq + EPS_F)
    return (volume[None, :], shell_fsc)


def solution(mesh):
    n_cls = mesh.shape["cls"]
    fine = jax.sharding.Mesh(
        mesh.devices.reshape(mesh.shape["half"], n_cls // X_CHIPS, X_CHIPS, mesh.shape["vol"]),
        ("half", "z", "x", "vol"),
    )
    rows = ("half", "z", "x")
    placed = (
        P(rows, "vol"),
        P(rows, None),
        P(CLS, "vol"),
        P(CLS, "vol"),
        P("vol", rows),
    )
    return jax.shard_map(
        shards,
        mesh=fine,
        in_specs=placed,
        out_specs=(P("vol", rows), P()),
        check_vma=False,
    )
```

```python
import functools

import jax
import jax.numpy as jnp
from jax import lax
from jax.experimental import pallas as pl
from jax.experimental.pallas import tpu as pltpu
from jax.sharding import PartitionSpec as P

IMG = 128
SHIFTS = 5
NSHELL = 128
PLANES = 4
VBOX = 256
VOXS = 262144


EPS_W = 1e-05
EPS_F = 1e-06

LO = 128
CLS = ("z", "x")
X_CHIPS = 4


def partner(shard, axis, apart):
    return lax.ppermute(shard, axis, [(i, i ^ 1 << apart) for i in range(lax.axis_size(axis))])


def digits_of(n):
    out, stride = [], 1
    while n % 4 == 0 and n > 1:
        out.append((stride, 4))
        stride, n = stride * 4, n // 4
    while n % 2 == 0 and n > 1:
        out.append((stride, 2))
        stride, n = stride * 2, n // 2
    return out


def shift_in_digit(x, axis, stride, radix, shift):
    n = lax.axis_size(axis)
    perm = []
    for i in range(n):
        d = (i // stride) % radix
        perm.append((i, i + ((d + shift) % radix - d) * stride))
    return lax.ppermute(x, axis, perm)


def butterfly_sum(x, axis):
    for bit in range(lax.axis_size(axis).bit_length() - 1):
        x = x + partner(x, axis, bit)
    return x


def exchange_sum(x, axis):
    n = lax.axis_size(axis)
    got = lax.all_to_all(jnp.broadcast_to(x[None], (n,) + x.shape), axis, 0, 0, tiled=True)
    total = got[0]
    for i in range(1, n):
        total = total + got[i]
    return total


def digit_sum(x, axis):
    me = lax.axis_index(axis)
    for stride, radix in digits_of(lax.axis_size(axis)):
        d = (me // stride) % radix
        got = jnp.stack([x] + [shift_in_digit(x, axis, stride, radix, s) for s in range(1, radix)])
        total = lax.dynamic_index_in_dim(got, d % radix, keepdims=False)
        for t in range(1, radix):
            total = total + lax.dynamic_index_in_dim(got, (d - t) % radix, keepdims=False)
        x = total
    return x


def exchange_rows(data, axis):
    n = lax.axis_size(axis)
    got = lax.all_to_all(jnp.moveaxis(data, 1, 0), axis, 0, 0, tiled=True)
    total = got[0]
    for i in range(1, n):
        total = total + got[i]
    return total


def reduce_scatter(x, inner, outer):
    n_inner = lax.axis_size(inner)
    n_outer = lax.axis_size(outer)
    a, _, length = x.shape
    data = exchange_rows(jnp.swapaxes(x.reshape(a, n_outer, n_inner, length), 1, 2), inner)
    return exchange_rows(data.reshape(a, n_outer, 1, length), outer)[:, 0]


def _project_kernel(w_ref, idx_ref, out_ref, wt_ref, it_ref):
    n = idx_ref.shape[0]
    hi_count = out_ref.shape[1]
    for shift_id in range(SHIFTS):
        wt_ref[shift_id] = w_ref[shift_id].T
    it_ref[...] = idx_ref[...].T
    lo_iota = lax.broadcasted_iota(jnp.int32, (LO, n), 0)
    hi_iota = lax.broadcasted_iota(jnp.int32, (hi_count, n), 0)

    def body(q, carry):
        v = wt_ref[0, pl.ds(lax.rem(q + SHIFTS // 2, IMG), 1), :]
        for shift_id in range(1, SHIFTS):
            row = lax.rem(q - (shift_id - SHIFTS // 2) + IMG, IMG)
            v = v + wt_ref[shift_id, pl.ds(row, 1), :]
        idx = it_ref[pl.ds(q, 1), :]
        lo = jnp.bitwise_and(idx, LO - 1)
        hi = jnp.right_shift(idx, 7)
        rt = jnp.where(lo == lo_iota, 1.0, 0.0).astype(jnp.bfloat16)
        vh = v.astype(jnp.bfloat16)
        vl = (v - vh.astype(jnp.float32)).astype(jnp.bfloat16)
        mask = hi == hi_iota
        zero = jnp.zeros((), jnp.bfloat16)
        lt = jnp.concatenate([jnp.where(mask, vh, zero), jnp.where(mask, vl, zero)], axis=0)
        o = lax.dot_general(lt, rt, (((1,), (1,)), ((), ())), preferred_element_type=jnp.float32)
        out_ref[q] = o[:hi_count] + o[hi_count:]
        return carry

    lax.fori_loop(0, IMG, body, 0, unroll=16)


def project(weighted, idx, bins):
    n, q_count = idx.shape
    hi_count = bins // LO
    return pl.pallas_call(
        _project_kernel,
        out_shape=jax.ShapeDtypeStruct((q_count, hi_count, LO), jnp.float32),
        in_specs=[
            pl.BlockSpec(memory_space=pltpu.VMEM),
            pl.BlockSpec(memory_space=pltpu.VMEM),
        ],
        out_specs=pl.BlockSpec(memory_space=pltpu.VMEM),
        scratch_shapes=[
            pltpu.VMEM((SHIFTS, q_count, n), jnp.float32),
            pltpu.VMEM((q_count, n), jnp.int32),
        ],
        cost_estimate=pl.CostEstimate(
            flops=2 * q_count * 2 * hi_count * LO * n,
            bytes_accessed=q_count * n * (4 * SHIFTS + 4) + q_count * bins * 4,
            transcendentals=0,
        ),
    )(weighted, idx)


def shards(images, groups, references, interp_index, shell_index):
    n_cls = lax.axis_size(CLS)
    n_vol = lax.axis_size("vol")
    n_half = lax.axis_size("half")
    part_count, pix_quarter = images.shape
    class_count = references.shape[0]
    capacity = max(2 * part_count // n_cls, 4)
    slot_count = n_cls * capacity
    owner_ids = groups[:, 0]
    matches = (owner_ids[:, None] == jnp.arange(n_cls, dtype=jnp.int32)[None, :]).astype(jnp.int32)
    order_in = jnp.sum(jnp.cumsum(matches, axis=0) * matches, axis=1) - 1
    slot_ids = owner_ids * capacity + order_in
    slot_hits = slot_ids[None, :] == jnp.arange(slot_count, dtype=jnp.int32)[:, None]
    quarter_rows = pix_quarter // IMG
    bins = VOXS // IMG
    outgoing = lax.dot_general(
        slot_hits.astype(jnp.bfloat16).reshape(n_cls, capacity, part_count),
        images.reshape(part_count, quarter_rows, IMG),
        (((2,), (0,)), ((), ())),
        preferred_element_type=jnp.float32,
    ).astype(jnp.bfloat16)
    arrived = lax.all_to_all(
        jnp.swapaxes(outgoing, 1, 2), CLS, split_axis=0, concat_axis=0, tiled=True
    )
    arrived = jnp.swapaxes(arrived, 1, 2).reshape(slot_count, quarter_rows, IMG)
    shaped_refs = references.reshape(class_count, quarter_rows, IMG)
    rolled_refs = jnp.concatenate(
        [jnp.roll(shaped_refs, -(shift_id - SHIFTS // 2), axis=2) for shift_id in range(SHIFTS)],
        axis=0,
    )
    partial_scores = lax.dot_general(
        arrived, rolled_refs, (((1, 2), (1, 2)), ((), ())), preferred_element_type=jnp.float32
    )
    partial_scores = partial_scores.reshape(slot_count, SHIFTS, class_count)
    scores = exchange_sum(partial_scores, "vol")
    squares = scores * scores
    mean_square = jnp.mean(squares, axis=(1, 2), keepdims=True)
    weights = (squares / (mean_square + EPS_W)).astype(jnp.bfloat16)
    weighted = lax.dot_general(
        weights.reshape(slot_count, SHIFTS * class_count),
        arrived,
        (((0,), (0,)), ((), ())),
        preferred_element_type=jnp.float32,
    )
    slab_part = project(
        weighted.reshape(SHIFTS, class_count * quarter_rows, IMG),
        interp_index.reshape(class_count * quarter_rows, IMG),
        bins,
    )
    piece_len = VOXS // (n_half * n_cls)
    slab_part = slab_part.reshape(n_half, n_cls, piece_len)
    own_block = reduce_scatter(slab_part, "x", "z").reshape(-1)
    half_id = lax.axis_index("half")
    other_block = partner(own_block, "half", 0)
    other_shell = partner(shell_index[0], "half", 0)
    first_block = jnp.where(half_id == 0, own_block, other_block)
    second_block = jnp.where(half_id == 0, other_block, own_block)
    shell_block = jnp.where(
        half_id == 0,
        jnp.concatenate([shell_index[0], other_shell]),
        jnp.concatenate([other_shell, shell_index[0]]),
    )
    block_hot = (shell_block[:, None] == jnp.arange(NSHELL, dtype=jnp.int32)[None, :]).astype(
        jnp.float32
    )
    stats = jnp.stack([first_block * first_block, second_block * second_block, first_block * second_block])
    shell_terms = jnp.dot(stats, block_hot, precision=lax.Precision.HIGHEST)
    shell_sums = exchange_sum(exchange_sum(shell_terms, "vol"), CLS)
    shell_fsc = shell_sums[2] / (jnp.sqrt(shell_sums[0]) * jnp.sqrt(shell_sums[1]) + EPS_F)
    mean_sq = (jnp.sum(shell_sums[0]) + jnp.sum(shell_sums[1]) + 2.0 * jnp.sum(shell_sums[2])) / (
        4.0 * n_vol * VOXS
    )
    first = lax.dynamic_index_in_dim(first_block.reshape(n_half, piece_len), half_id, keepdims=False)
    second = lax.dynamic_index_in_dim(second_block.reshape(n_half, piece_len), half_id, keepdims=False)
    shell_hot = (shell_index[0][:, None] == jnp.arange(NSHELL, dtype=jnp.int32)[None, :]).astype(
        jnp.float32
    )
    filter_vox = jnp.dot(shell_hot, shell_fsc, precision=lax.Precision.HIGHEST)
    volume = filter_vox * (0.5 * (first + second)) / jnp.sqrt(mean_sq + EPS_F)
    return (volume[None, :], shell_fsc)


def solution(mesh):
    n_cls = mesh.shape["cls"]
    fine = jax.sharding.Mesh(
        mesh.devices.reshape(mesh.shape["half"], n_cls // X_CHIPS, X_CHIPS, mesh.shape["vol"]),
        ("half", "z", "x", "vol"),
    )
    rows = ("half", "z", "x")
    placed = (
        P(rows, "vol"),
        P(rows, None),
        P(CLS, "vol"),
        P(CLS, "vol"),
        P("vol", rows),
    )
    return jax.shard_map(
        shards,
        mesh=fine,
        in_specs=placed,
        out_specs=(P("vol", rows), P()),
        check_vma=False,
    )
```

```python
import functools

import jax
import jax.numpy as jnp
from jax import lax
from jax.experimental import pallas as pl
from jax.experimental.pallas import tpu as pltpu
from jax.sharding import PartitionSpec as P

IMG = 128
SHIFTS = 5
NSHELL = 128
PLANES = 4
VBOX = 256
VOXS = 262144


EPS_W = 1e-05
EPS_F = 1e-06

LO = 128
CLS = ("z", "x")
X_CHIPS = 4


def partner(shard, axis, apart):
    return lax.ppermute(shard, axis, [(i, i ^ 1 << apart) for i in range(lax.axis_size(axis))])


def digits_of(n):
    out, stride = [], 1
    while n % 4 == 0 and n > 1:
        out.append((stride, 4))
        stride, n = stride * 4, n // 4
    while n % 2 == 0 and n > 1:
        out.append((stride, 2))
        stride, n = stride * 2, n // 2
    return out


def shift_in_digit(x, axis, stride, radix, shift):
    n = lax.axis_size(axis)
    perm = []
    for i in range(n):
        d = (i // stride) % radix
        perm.append((i, i + ((d + shift) % radix - d) * stride))
    return lax.ppermute(x, axis, perm)


def butterfly_sum(x, axis):
    for bit in range(lax.axis_size(axis).bit_length() - 1):
        x = x + partner(x, axis, bit)
    return x


def exchange_sum(x, axis):
    n = lax.axis_size(axis)
    got = lax.all_to_all(jnp.broadcast_to(x[None], (n,) + x.shape), axis, 0, 0, tiled=True)
    total = got[0]
    for i in range(1, n):
        total = total + got[i]
    return total


def digit_sum(x, axis):
    me = lax.axis_index(axis)
    for stride, radix in digits_of(lax.axis_size(axis)):
        d = (me // stride) % radix
        got = jnp.stack([x] + [shift_in_digit(x, axis, stride, radix, s) for s in range(1, radix)])
        total = lax.dynamic_index_in_dim(got, d % radix, keepdims=False)
        for t in range(1, radix):
            total = total + lax.dynamic_index_in_dim(got, (d - t) % radix, keepdims=False)
        x = total
    return x


def exchange_rows(data, axis):
    n = lax.axis_size(axis)
    got = lax.all_to_all(jnp.moveaxis(data, 1, 0), axis, 0, 0, tiled=True)
    total = got[0]
    for i in range(1, n):
        total = total + got[i]
    return total


def reduce_scatter(x, inner, outer):
    n_inner = lax.axis_size(inner)
    n_outer = lax.axis_size(outer)
    a, _, length = x.shape
    data = exchange_rows(jnp.swapaxes(x.reshape(a, n_outer, n_inner, length), 1, 2), inner)
    return exchange_rows(data.reshape(a, n_outer, 1, length), outer)[:, 0]


def _project_kernel(w_ref, idx_ref, out_ref, wt_ref, it_ref):
    n = idx_ref.shape[0]
    hi_count = out_ref.shape[1]
    for shift_id in range(SHIFTS):
        wt_ref[shift_id] = w_ref[shift_id].T
    it_ref[...] = idx_ref[...].T
    lo_iota = lax.broadcasted_iota(jnp.int32, (LO, n), 0)
    hi_iota = lax.broadcasted_iota(jnp.int32, (hi_count, n), 0)

    def body(q, carry):
        v = wt_ref[0, pl.ds(lax.rem(q + SHIFTS // 2, IMG), 1), :]
        for shift_id in range(1, SHIFTS):
            row = lax.rem(q - (shift_id - SHIFTS // 2) + IMG, IMG)
            v = v + wt_ref[shift_id, pl.ds(row, 1), :]
        idx = it_ref[pl.ds(q, 1), :]
        lo = jnp.bitwise_and(idx, LO - 1)
        hi = jnp.right_shift(idx, 7)
        rt = jnp.where(lo == lo_iota, 1.0, 0.0).astype(jnp.bfloat16)
        vh = v.astype(jnp.bfloat16)
        vl = (v - vh.astype(jnp.float32)).astype(jnp.bfloat16)
        mask = hi == hi_iota
        zero = jnp.zeros((), jnp.bfloat16)
        lt = jnp.concatenate([jnp.where(mask, vh, zero), jnp.where(mask, vl, zero)], axis=0)
        o = lax.dot_general(lt, rt, (((1,), (1,)), ((), ())), preferred_element_type=jnp.float32)
        out_ref[q] = o[:hi_count] + o[hi_count:]
        return carry

    lax.fori_loop(0, IMG, body, 0, unroll=32)


def project(weighted, idx, bins):
    n, q_count = idx.shape
    hi_count = bins // LO
    return pl.pallas_call(
        _project_kernel,
        out_shape=jax.ShapeDtypeStruct((q_count, hi_count, LO), jnp.float32),
        in_specs=[
            pl.BlockSpec(memory_space=pltpu.VMEM),
            pl.BlockSpec(memory_space=pltpu.VMEM),
        ],
        out_specs=pl.BlockSpec(memory_space=pltpu.VMEM),
        scratch_shapes=[
            pltpu.VMEM((SHIFTS, q_count, n), jnp.float32),
            pltpu.VMEM((q_count, n), jnp.int32),
        ],
        cost_estimate=pl.CostEstimate(
            flops=2 * q_count * 2 * hi_count * LO * n,
            bytes_accessed=q_count * n * (4 * SHIFTS + 4) + q_count * bins * 4,
            transcendentals=0,
        ),
    )(weighted, idx)


def shards(images, groups, references, interp_index, shell_index):
    n_cls = lax.axis_size(CLS)
    n_vol = lax.axis_size("vol")
    n_half = lax.axis_size("half")
    part_count, pix_quarter = images.shape
    class_count = references.shape[0]
    capacity = max(2 * part_count // n_cls, 4)
    slot_count = n_cls * capacity
    owner_ids = groups[:, 0]
    matches = (owner_ids[:, None] == jnp.arange(n_cls, dtype=jnp.int32)[None, :]).astype(jnp.int32)
    order_in = jnp.sum(jnp.cumsum(matches, axis=0) * matches, axis=1) - 1
    slot_ids = owner_ids * capacity + order_in
    slot_hits = slot_ids[None, :] == jnp.arange(slot_count, dtype=jnp.int32)[:, None]
    quarter_rows = pix_quarter // IMG
    bins = VOXS // IMG
    outgoing = lax.dot_general(
        slot_hits.astype(jnp.bfloat16).reshape(n_cls, capacity, part_count),
        images.reshape(part_count, quarter_rows, IMG),
        (((2,), (0,)), ((), ())),
        preferred_element_type=jnp.float32,
    ).astype(jnp.bfloat16)
    arrived = lax.all_to_all(
        jnp.swapaxes(outgoing, 1, 2), CLS, split_axis=0, concat_axis=0, tiled=True
    )
    arrived = jnp.swapaxes(arrived, 1, 2).reshape(slot_count, quarter_rows, IMG)
    shaped_refs = references.reshape(class_count, quarter_rows, IMG)
    rolled_refs = jnp.concatenate(
        [jnp.roll(shaped_refs, -(shift_id - SHIFTS // 2), axis=2) for shift_id in range(SHIFTS)],
        axis=0,
    )
    partial_scores = lax.dot_general(
        arrived, rolled_refs, (((1, 2), (1, 2)), ((), ())), preferred_element_type=jnp.float32
    )
    partial_scores = partial_scores.reshape(slot_count, SHIFTS, class_count)
    scores = exchange_sum(partial_scores, "vol")
    squares = scores * scores
    mean_square = jnp.mean(squares, axis=(1, 2), keepdims=True)
    weights = (squares / (mean_square + EPS_W)).astype(jnp.bfloat16)
    weighted = lax.dot_general(
        weights.reshape(slot_count, SHIFTS * class_count),
        arrived,
        (((0,), (0,)), ((), ())),
        preferred_element_type=jnp.float32,
    )
    slab_part = project(
        weighted.reshape(SHIFTS, class_count * quarter_rows, IMG),
        interp_index.reshape(class_count * quarter_rows, IMG),
        bins,
    )
    piece_len = VOXS // (n_half * n_cls)
    slab_part = slab_part.reshape(n_half, n_cls, piece_len)
    own_block = reduce_scatter(slab_part, "x", "z").reshape(-1)
    half_id = lax.axis_index("half")
    other_block = partner(own_block, "half", 0)
    other_shell = partner(shell_index[0], "half", 0)
    first_block = jnp.where(half_id == 0, own_block, other_block)
    second_block = jnp.where(half_id == 0, other_block, own_block)
    shell_block = jnp.where(
        half_id == 0,
        jnp.concatenate([shell_index[0], other_shell]),
        jnp.concatenate([other_shell, shell_index[0]]),
    )
    block_hot = (shell_block[:, None] == jnp.arange(NSHELL, dtype=jnp.int32)[None, :]).astype(
        jnp.float32
    )
    stats = jnp.stack([first_block * first_block, second_block * second_block, first_block * second_block])
    shell_terms = jnp.dot(stats, block_hot, precision=lax.Precision.HIGHEST)
    shell_sums = exchange_sum(exchange_sum(shell_terms, "vol"), CLS)
    shell_fsc = shell_sums[2] / (jnp.sqrt(shell_sums[0]) * jnp.sqrt(shell_sums[1]) + EPS_F)
    mean_sq = (jnp.sum(shell_sums[0]) + jnp.sum(shell_sums[1]) + 2.0 * jnp.sum(shell_sums[2])) / (
        4.0 * n_vol * VOXS
    )
    first = lax.dynamic_index_in_dim(first_block.reshape(n_half, piece_len), half_id, keepdims=False)
    second = lax.dynamic_index_in_dim(second_block.reshape(n_half, piece_len), half_id, keepdims=False)
    shell_hot = (shell_index[0][:, None] == jnp.arange(NSHELL, dtype=jnp.int32)[None, :]).astype(
        jnp.float32
    )
    filter_vox = jnp.dot(shell_hot, shell_fsc, precision=lax.Precision.HIGHEST)
    volume = filter_vox * (0.5 * (first + second)) / jnp.sqrt(mean_sq + EPS_F)
    return (volume[None, :], shell_fsc)


def solution(mesh):
    n_cls = mesh.shape["cls"]
    fine = jax.sharding.Mesh(
        mesh.devices.reshape(mesh.shape["half"], n_cls // X_CHIPS, X_CHIPS, mesh.shape["vol"]),
        ("half", "z", "x", "vol"),
    )
    rows = ("half", "z", "x")
    placed = (
        P(rows, "vol"),
        P(rows, None),
        P(CLS, "vol"),
        P(CLS, "vol"),
        P("vol", rows),
    )
    return jax.shard_map(
        shards,
        mesh=fine,
        in_specs=placed,
        out_specs=(P("vol", rows), P()),
        check_vma=False,
    )
```

```python
import functools

import jax
import jax.numpy as jnp
from jax import lax
from jax.experimental import pallas as pl
from jax.experimental.pallas import tpu as pltpu
from jax.sharding import PartitionSpec as P

IMG = 128
SHIFTS = 5
NSHELL = 128
PLANES = 4
VBOX = 256
VOXS = 262144


EPS_W = 1e-05
EPS_F = 1e-06

LO = 128
CLS = ("z", "x")
X_CHIPS = 4


def partner(shard, axis, apart):
    return lax.ppermute(shard, axis, [(i, i ^ 1 << apart) for i in range(lax.axis_size(axis))])


def digits_of(n):
    out, stride = [], 1
    while n % 4 == 0 and n > 1:
        out.append((stride, 4))
        stride, n = stride * 4, n // 4
    while n % 2 == 0 and n > 1:
        out.append((stride, 2))
        stride, n = stride * 2, n // 2
    return out


def shift_in_digit(x, axis, stride, radix, shift):
    n = lax.axis_size(axis)
    perm = []
    for i in range(n):
        d = (i // stride) % radix
        perm.append((i, i + ((d + shift) % radix - d) * stride))
    return lax.ppermute(x, axis, perm)


def butterfly_sum(x, axis):
    for bit in range(lax.axis_size(axis).bit_length() - 1):
        x = x + partner(x, axis, bit)
    return x


def exchange_sum(x, axis):
    n = lax.axis_size(axis)
    got = lax.all_to_all(jnp.broadcast_to(x[None], (n,) + x.shape), axis, 0, 0, tiled=True)
    total = got[0]
    for i in range(1, n):
        total = total + got[i]
    return total


def digit_sum(x, axis):
    me = lax.axis_index(axis)
    for stride, radix in digits_of(lax.axis_size(axis)):
        d = (me // stride) % radix
        got = jnp.stack([x] + [shift_in_digit(x, axis, stride, radix, s) for s in range(1, radix)])
        total = lax.dynamic_index_in_dim(got, d % radix, keepdims=False)
        for t in range(1, radix):
            total = total + lax.dynamic_index_in_dim(got, (d - t) % radix, keepdims=False)
        x = total
    return x


def exchange_rows(data, axis):
    n = lax.axis_size(axis)
    got = lax.all_to_all(jnp.moveaxis(data, 1, 0), axis, 0, 0, tiled=True)
    total = got[0]
    for i in range(1, n):
        total = total + got[i]
    return total


def reduce_scatter(x, inner, outer):
    n_inner = lax.axis_size(inner)
    n_outer = lax.axis_size(outer)
    a, _, length = x.shape
    data = exchange_rows(jnp.swapaxes(x.reshape(a, n_outer, n_inner, length), 1, 2), inner)
    return exchange_rows(data.reshape(a, n_outer, 1, length), outer)[:, 0]


def _project_kernel(w_ref, idx_ref, out_ref, wt_ref, it_ref):
    n = idx_ref.shape[0]
    hi_count = out_ref.shape[1]
    for shift_id in range(SHIFTS):
        wt_ref[shift_id] = w_ref[shift_id].T
    it_ref[...] = idx_ref[...].T
    lo_iota = lax.broadcasted_iota(jnp.int32, (LO, n), 0)
    hi_iota = lax.broadcasted_iota(jnp.int32, (hi_count, n), 0)

    def body(q, carry):
        v = wt_ref[0, pl.ds(lax.rem(q + SHIFTS // 2, IMG), 1), :]
        for shift_id in range(1, SHIFTS):
            row = lax.rem(q - (shift_id - SHIFTS // 2) + IMG, IMG)
            v = v + wt_ref[shift_id, pl.ds(row, 1), :]
        idx = it_ref[pl.ds(q, 1), :]
        lo = jnp.bitwise_and(idx, LO - 1)
        hi = jnp.right_shift(idx, 7)
        rt = jnp.where(lo == lo_iota, 1.0, 0.0).astype(jnp.bfloat16)
        vh = v.astype(jnp.bfloat16)
        vl = (v - vh.astype(jnp.float32)).astype(jnp.bfloat16)
        mask = hi == hi_iota
        zero = jnp.zeros((), jnp.bfloat16)
        lt = jnp.concatenate([jnp.where(mask, vh, zero), jnp.where(mask, vl, zero)], axis=0)
        o = lax.dot_general(lt, rt, (((1,), (1,)), ((), ())), preferred_element_type=jnp.float32)
        out_ref[q] = o[:hi_count] + o[hi_count:]
        return carry

    lax.fori_loop(0, IMG, body, 0, unroll=64)


def project(weighted, idx, bins):
    n, q_count = idx.shape
    hi_count = bins // LO
    return pl.pallas_call(
        _project_kernel,
        out_shape=jax.ShapeDtypeStruct((q_count, hi_count, LO), jnp.float32),
        in_specs=[
            pl.BlockSpec(memory_space=pltpu.VMEM),
            pl.BlockSpec(memory_space=pltpu.VMEM),
        ],
        out_specs=pl.BlockSpec(memory_space=pltpu.VMEM),
        scratch_shapes=[
            pltpu.VMEM((SHIFTS, q_count, n), jnp.float32),
            pltpu.VMEM((q_count, n), jnp.int32),
        ],
        cost_estimate=pl.CostEstimate(
            flops=2 * q_count * 2 * hi_count * LO * n,
            bytes_accessed=q_count * n * (4 * SHIFTS + 4) + q_count * bins * 4,
            transcendentals=0,
        ),
    )(weighted, idx)


def shards(images, groups, references, interp_index, shell_index):
    n_cls = lax.axis_size(CLS)
    n_vol = lax.axis_size("vol")
    n_half = lax.axis_size("half")
    part_count, pix_quarter = images.shape
    class_count = references.shape[0]
    capacity = max(2 * part_count // n_cls, 4)
    slot_count = n_cls * capacity
    owner_ids = groups[:, 0]
    matches = (owner_ids[:, None] == jnp.arange(n_cls, dtype=jnp.int32)[None, :]).astype(jnp.int32)
    order_in = jnp.sum(jnp.cumsum(matches, axis=0) * matches, axis=1) - 1
    slot_ids = owner_ids * capacity + order_in
    slot_hits = slot_ids[None, :] == jnp.arange(slot_count, dtype=jnp.int32)[:, None]
    quarter_rows = pix_quarter // IMG
    bins = VOXS // IMG
    outgoing = lax.dot_general(
        slot_hits.astype(jnp.bfloat16).reshape(n_cls, capacity, part_count),
        images.reshape(part_count, quarter_rows, IMG),
        (((2,), (0,)), ((), ())),
        preferred_element_type=jnp.float32,
    ).astype(jnp.bfloat16)
    arrived = lax.all_to_all(
        jnp.swapaxes(outgoing, 1, 2), CLS, split_axis=0, concat_axis=0, tiled=True
    )
    arrived = jnp.swapaxes(arrived, 1, 2).reshape(slot_count, quarter_rows, IMG)
    shaped_refs = references.reshape(class_count, quarter_rows, IMG)
    rolled_refs = jnp.concatenate(
        [jnp.roll(shaped_refs, -(shift_id - SHIFTS // 2), axis=2) for shift_id in range(SHIFTS)],
        axis=0,
    )
    partial_scores = lax.dot_general(
        arrived, rolled_refs, (((1, 2), (1, 2)), ((), ())), preferred_element_type=jnp.float32
    )
    partial_scores = partial_scores.reshape(slot_count, SHIFTS, class_count)
    scores = exchange_sum(partial_scores, "vol")
    squares = scores * scores
    mean_square = jnp.mean(squares, axis=(1, 2), keepdims=True)
    weights = (squares / (mean_square + EPS_W)).astype(jnp.bfloat16)
    weighted = lax.dot_general(
        weights.reshape(slot_count, SHIFTS * class_count),
        arrived,
        (((0,), (0,)), ((), ())),
        preferred_element_type=jnp.float32,
    )
    slab_part = project(
        weighted.reshape(SHIFTS, class_count * quarter_rows, IMG),
        interp_index.reshape(class_count * quarter_rows, IMG),
        bins,
    )
    piece_len = VOXS // (n_half * n_cls)
    slab_part = slab_part.reshape(n_half, n_cls, piece_len)
    own_block = reduce_scatter(slab_part, "x", "z").reshape(-1)
    half_id = lax.axis_index("half")
    other_block = partner(own_block, "half", 0)
    other_shell = partner(shell_index[0], "half", 0)
    first_block = jnp.where(half_id == 0, own_block, other_block)
    second_block = jnp.where(half_id == 0, other_block, own_block)
    shell_block = jnp.where(
        half_id == 0,
        jnp.concatenate([shell_index[0], other_shell]),
        jnp.concatenate([other_shell, shell_index[0]]),
    )
    block_hot = (shell_block[:, None] == jnp.arange(NSHELL, dtype=jnp.int32)[None, :]).astype(
        jnp.float32
    )
    stats = jnp.stack([first_block * first_block, second_block * second_block, first_block * second_block])
    shell_terms = jnp.dot(stats, block_hot, precision=lax.Precision.HIGHEST)
    shell_sums = exchange_sum(exchange_sum(shell_terms, "vol"), CLS)
    shell_fsc = shell_sums[2] / (jnp.sqrt(shell_sums[0]) * jnp.sqrt(shell_sums[1]) + EPS_F)
    mean_sq = (jnp.sum(shell_sums[0]) + jnp.sum(shell_sums[1]) + 2.0 * jnp.sum(shell_sums[2])) / (
        4.0 * n_vol * VOXS
    )
    first = lax.dynamic_index_in_dim(first_block.reshape(n_half, piece_len), half_id, keepdims=False)
    second = lax.dynamic_index_in_dim(second_block.reshape(n_half, piece_len), half_id, keepdims=False)
    shell_hot = (shell_index[0][:, None] == jnp.arange(NSHELL, dtype=jnp.int32)[None, :]).astype(
        jnp.float32
    )
    filter_vox = jnp.dot(shell_hot, shell_fsc, precision=lax.Precision.HIGHEST)
    volume = filter_vox * (0.5 * (first + second)) / jnp.sqrt(mean_sq + EPS_F)
    return (volume[None, :], shell_fsc)


def solution(mesh):
    n_cls = mesh.shape["cls"]
    fine = jax.sharding.Mesh(
        mesh.devices.reshape(mesh.shape["half"], n_cls // X_CHIPS, X_CHIPS, mesh.shape["vol"]),
        ("half", "z", "x", "vol"),
    )
    rows = ("half", "z", "x")
    placed = (
        P(rows, "vol"),
        P(rows, None),
        P(CLS, "vol"),
        P(CLS, "vol"),
        P("vol", rows),
    )
    return jax.shard_map(
        shards,
        mesh=fine,
        in_specs=placed,
        out_specs=(P("vol", rows), P()),
        check_vma=False,
    )
```

```python
import functools

import jax
import jax.numpy as jnp
from jax import lax
from jax.experimental import pallas as pl
from jax.experimental.pallas import tpu as pltpu
from jax.sharding import PartitionSpec as P

IMG = 128
SHIFTS = 5
NSHELL = 128
PLANES = 4
VBOX = 256
VOXS = 262144


EPS_W = 1e-05
EPS_F = 1e-06

LO = 128
CLS = ("z", "x")
X_CHIPS = 4


def partner(shard, axis, apart):
    return lax.ppermute(shard, axis, [(i, i ^ 1 << apart) for i in range(lax.axis_size(axis))])


def digits_of(n):
    out, stride = [], 1
    while n % 4 == 0 and n > 1:
        out.append((stride, 4))
        stride, n = stride * 4, n // 4
    while n % 2 == 0 and n > 1:
        out.append((stride, 2))
        stride, n = stride * 2, n // 2
    return out


def shift_in_digit(x, axis, stride, radix, shift):
    n = lax.axis_size(axis)
    perm = []
    for i in range(n):
        d = (i // stride) % radix
        perm.append((i, i + ((d + shift) % radix - d) * stride))
    return lax.ppermute(x, axis, perm)


def butterfly_sum(x, axis):
    for bit in range(lax.axis_size(axis).bit_length() - 1):
        x = x + partner(x, axis, bit)
    return x


def exchange_sum(x, axis):
    n = lax.axis_size(axis)
    got = lax.all_to_all(jnp.broadcast_to(x[None], (n,) + x.shape), axis, 0, 0, tiled=True)
    total = got[0]
    for i in range(1, n):
        total = total + got[i]
    return total


def digit_sum(x, axis):
    me = lax.axis_index(axis)
    for stride, radix in digits_of(lax.axis_size(axis)):
        d = (me // stride) % radix
        got = jnp.stack([x] + [shift_in_digit(x, axis, stride, radix, s) for s in range(1, radix)])
        total = lax.dynamic_index_in_dim(got, d % radix, keepdims=False)
        for t in range(1, radix):
            total = total + lax.dynamic_index_in_dim(got, (d - t) % radix, keepdims=False)
        x = total
    return x


def exchange_rows(data, axis):
    n = lax.axis_size(axis)
    got = lax.all_to_all(jnp.moveaxis(data, 1, 0), axis, 0, 0, tiled=True)
    total = got[0]
    for i in range(1, n):
        total = total + got[i]
    return total


def reduce_scatter(x, inner, outer):
    n_inner = lax.axis_size(inner)
    n_outer = lax.axis_size(outer)
    a, _, length = x.shape
    data = exchange_rows(jnp.swapaxes(x.reshape(a, n_outer, n_inner, length), 1, 2), inner)
    return exchange_rows(data.reshape(a, n_outer, 1, length), outer)[:, 0]


def _project_kernel(w_ref, idx_ref, out_ref, wt_ref, it_ref):
    n = idx_ref.shape[0]
    hi_count = out_ref.shape[1]
    for shift_id in range(SHIFTS):
        wt_ref[shift_id] = w_ref[shift_id].T
    it_ref[...] = idx_ref[...].T
    lo_iota = lax.broadcasted_iota(jnp.int32, (LO, n), 0)
    hi_iota = lax.broadcasted_iota(jnp.int32, (hi_count, n), 0)

    def body(q, carry):
        v = wt_ref[0, pl.ds(lax.rem(q + SHIFTS // 2, IMG), 1), :]
        for shift_id in range(1, SHIFTS):
            row = lax.rem(q - (shift_id - SHIFTS // 2) + IMG, IMG)
            v = v + wt_ref[shift_id, pl.ds(row, 1), :]
        idx = it_ref[pl.ds(q, 1), :]
        lo = jnp.bitwise_and(idx, LO - 1)
        hi = jnp.right_shift(idx, 7)
        rt = jnp.where(lo == lo_iota, 1.0, 0.0).astype(jnp.bfloat16)
        vh = v.astype(jnp.bfloat16)
        vl = (v - vh.astype(jnp.float32)).astype(jnp.bfloat16)
        mask = hi == hi_iota
        zero = jnp.zeros((), jnp.bfloat16)
        lt = jnp.concatenate([jnp.where(mask, vh, zero), jnp.where(mask, vl, zero)], axis=0)
        o = lax.dot_general(lt, rt, (((1,), (1,)), ((), ())), preferred_element_type=jnp.float32)
        out_ref[q] = o[:hi_count] + o[hi_count:]
        return carry

    lax.fori_loop(0, IMG, body, 0, unroll=64)


def project(weighted, idx, bins):
    n, q_count = idx.shape
    hi_count = bins // LO
    return pl.pallas_call(
        _project_kernel,
        out_shape=jax.ShapeDtypeStruct((q_count, hi_count, LO), jnp.float32),
        in_specs=[
            pl.BlockSpec(memory_space=pltpu.VMEM),
            pl.BlockSpec(memory_space=pltpu.VMEM),
        ],
        out_specs=pl.BlockSpec(memory_space=pltpu.VMEM),
        scratch_shapes=[
            pltpu.VMEM((SHIFTS, q_count, n), jnp.float32),
            pltpu.VMEM((q_count, n), jnp.int32),
        ],
        cost_estimate=pl.CostEstimate(
            flops=2 * q_count * 2 * hi_count * LO * n,
            bytes_accessed=q_count * n * (4 * SHIFTS + 4) + q_count * bins * 4,
            transcendentals=0,
        ),
    )(weighted, idx)


def shards(images, groups, references, interp_index, shell_index):
    n_cls = lax.axis_size(CLS)
    n_vol = lax.axis_size("vol")
    n_half = lax.axis_size("half")
    part_count, pix_quarter = images.shape
    class_count = references.shape[0]
    capacity = max(2 * part_count // n_cls, 4)
    slot_count = n_cls * capacity
    owner_ids = groups[:, 0]
    matches = (owner_ids[:, None] == jnp.arange(n_cls, dtype=jnp.int32)[None, :]).astype(jnp.int32)
    order_in = jnp.sum(jnp.cumsum(matches, axis=0) * matches, axis=1) - 1
    slot_ids = owner_ids * capacity + order_in
    slot_hits = slot_ids[None, :] == jnp.arange(slot_count, dtype=jnp.int32)[:, None]
    quarter_rows = pix_quarter // IMG
    bins = VOXS // IMG
    outgoing = lax.dot_general(
        slot_hits.astype(jnp.bfloat16).reshape(n_cls, capacity, part_count),
        images.reshape(part_count, quarter_rows, IMG),
        (((2,), (0,)), ((), ())),
        preferred_element_type=jnp.float32,
    ).astype(jnp.bfloat16)
    arrived = lax.all_to_all(
        jnp.swapaxes(outgoing, 1, 2), CLS, split_axis=0, concat_axis=0, tiled=True
    )
    arrived = jnp.swapaxes(arrived, 1, 2).reshape(slot_count, quarter_rows, IMG)
    shaped_refs = references.reshape(class_count, quarter_rows, IMG)
    rolled_refs = jnp.concatenate(
        [jnp.roll(shaped_refs, -(shift_id - SHIFTS // 2), axis=2) for shift_id in range(SHIFTS)],
        axis=0,
    )
    partial_scores = lax.dot_general(
        arrived, rolled_refs, (((1, 2), (1, 2)), ((), ())), preferred_element_type=jnp.float32
    )
    partial_scores = partial_scores.reshape(slot_count, SHIFTS, class_count)
    scores = exchange_sum(partial_scores, "vol")
    squares = scores * scores
    mean_square = jnp.mean(squares, axis=(1, 2), keepdims=True)
    weights = (squares / (mean_square + EPS_W)).astype(jnp.bfloat16)
    weighted = lax.dot_general(
        weights.reshape(slot_count, SHIFTS * class_count),
        arrived,
        (((0,), (0,)), ((), ())),
        preferred_element_type=jnp.float32,
    )
    slab_part = project(
        weighted.reshape(SHIFTS, class_count * quarter_rows, IMG),
        interp_index.reshape(class_count * quarter_rows, IMG),
        bins,
    )
    piece_len = VOXS // (n_half * n_cls)
    slab_part = slab_part.reshape(n_half, n_cls, piece_len)
    own_block = reduce_scatter(slab_part, "x", "z").reshape(-1)
    half_id = lax.axis_index("half")
    other_block = partner(own_block, "half", 0)
    other_shell = partner(shell_index[0], "half", 0)
    first_block = jnp.where(half_id == 0, own_block, other_block)
    second_block = jnp.where(half_id == 0, other_block, own_block)
    shell_block = jnp.where(
        half_id == 0,
        jnp.concatenate([shell_index[0], other_shell]),
        jnp.concatenate([other_shell, shell_index[0]]),
    )
    block_hot = (shell_block[:, None] == jnp.arange(NSHELL, dtype=jnp.int32)[None, :]).astype(
        jnp.float32
    )
    stats = jnp.stack([first_block * first_block, second_block * second_block, first_block * second_block])
    shell_terms = jnp.dot(stats, block_hot, precision=lax.Precision.HIGHEST)
    shell_sums = exchange_sum(exchange_sum(shell_terms, CLS), "vol")
    shell_fsc = shell_sums[2] / (jnp.sqrt(shell_sums[0]) * jnp.sqrt(shell_sums[1]) + EPS_F)
    mean_sq = (jnp.sum(shell_sums[0]) + jnp.sum(shell_sums[1]) + 2.0 * jnp.sum(shell_sums[2])) / (
        4.0 * n_vol * VOXS
    )
    first = lax.dynamic_index_in_dim(first_block.reshape(n_half, piece_len), half_id, keepdims=False)
    second = lax.dynamic_index_in_dim(second_block.reshape(n_half, piece_len), half_id, keepdims=False)
    shell_hot = (shell_index[0][:, None] == jnp.arange(NSHELL, dtype=jnp.int32)[None, :]).astype(
        jnp.float32
    )
    filter_vox = jnp.dot(shell_hot, shell_fsc, precision=lax.Precision.HIGHEST)
    volume = filter_vox * (0.5 * (first + second)) / jnp.sqrt(mean_sq + EPS_F)
    return (volume[None, :], shell_fsc)


def solution(mesh):
    n_cls = mesh.shape["cls"]
    fine = jax.sharding.Mesh(
        mesh.devices.reshape(mesh.shape["half"], n_cls // X_CHIPS, X_CHIPS, mesh.shape["vol"]),
        ("half", "z", "x", "vol"),
    )
    rows = ("half", "z", "x")
    placed = (
        P(rows, "vol"),
        P(rows, None),
        P(CLS, "vol"),
        P(CLS, "vol"),
        P("vol", rows),
    )
    return jax.shard_map(
        shards,
        mesh=fine,
        in_specs=placed,
        out_specs=(P("vol", rows), P()),
        check_vma=False,
    )
```

```python
import functools

import jax
import jax.numpy as jnp
from jax import lax
from jax.experimental import pallas as pl
from jax.experimental.pallas import tpu as pltpu
from jax.sharding import PartitionSpec as P

IMG = 128
SHIFTS = 5
NSHELL = 128
PLANES = 4
VBOX = 256
VOXS = 262144


EPS_W = 1e-05
EPS_F = 1e-06

LO = 128
CLS = ("z", "x")
X_CHIPS = 4


def partner(shard, axis, apart):
    return lax.ppermute(shard, axis, [(i, i ^ 1 << apart) for i in range(lax.axis_size(axis))])


def digits_of(n):
    out, stride = [], 1
    while n % 4 == 0 and n > 1:
        out.append((stride, 4))
        stride, n = stride * 4, n // 4
    while n % 2 == 0 and n > 1:
        out.append((stride, 2))
        stride, n = stride * 2, n // 2
    return out


def shift_in_digit(x, axis, stride, radix, shift):
    n = lax.axis_size(axis)
    perm = []
    for i in range(n):
        d = (i // stride) % radix
        perm.append((i, i + ((d + shift) % radix - d) * stride))
    return lax.ppermute(x, axis, perm)


def butterfly_sum(x, axis):
    for bit in range(lax.axis_size(axis).bit_length() - 1):
        x = x + partner(x, axis, bit)
    return x


def exchange_sum(x, axis):
    n = lax.axis_size(axis)
    got = lax.all_to_all(jnp.broadcast_to(x[None], (n,) + x.shape), axis, 0, 0, tiled=True)
    total = got[0]
    for i in range(1, n):
        total = total + got[i]
    return total


def digit_sum(x, axis):
    me = lax.axis_index(axis)
    for stride, radix in digits_of(lax.axis_size(axis)):
        d = (me // stride) % radix
        got = jnp.stack([x] + [shift_in_digit(x, axis, stride, radix, s) for s in range(1, radix)])
        total = lax.dynamic_index_in_dim(got, d % radix, keepdims=False)
        for t in range(1, radix):
            total = total + lax.dynamic_index_in_dim(got, (d - t) % radix, keepdims=False)
        x = total
    return x


def exchange_rows(data, axis):
    n = lax.axis_size(axis)
    got = lax.all_to_all(jnp.moveaxis(data, 1, 0), axis, 0, 0, tiled=True)
    total = got[0]
    for i in range(1, n):
        total = total + got[i]
    return total


def reduce_scatter(x, inner, outer):
    n_inner = lax.axis_size(inner)
    n_outer = lax.axis_size(outer)
    a, _, length = x.shape
    data = exchange_rows(jnp.swapaxes(x.reshape(a, n_outer, n_inner, length), 1, 2), inner)
    return exchange_rows(data.reshape(a, n_outer, 1, length), outer)[:, 0]


def _project_kernel(w_ref, idx_ref, out_ref, wt_ref, it_ref):
    n = idx_ref.shape[0]
    hi_count = out_ref.shape[1]
    for shift_id in range(SHIFTS):
        wt_ref[shift_id] = w_ref[shift_id].T
    it_ref[...] = idx_ref[...].T
    lo_iota = lax.broadcasted_iota(jnp.int32, (LO, n), 0)
    hi_iota = lax.broadcasted_iota(jnp.int32, (hi_count, n), 0)

    def body(q, carry):
        v = wt_ref[0, pl.ds(lax.rem(q + SHIFTS // 2, IMG), 1), :]
        for shift_id in range(1, SHIFTS):
            row = lax.rem(q - (shift_id - SHIFTS // 2) + IMG, IMG)
            v = v + wt_ref[shift_id, pl.ds(row, 1), :]
        idx = it_ref[pl.ds(q, 1), :]
        lo = jnp.bitwise_and(idx, LO - 1)
        hi = jnp.right_shift(idx, 7)
        rt = jnp.where(lo == lo_iota, 1.0, 0.0).astype(jnp.bfloat16)
        vh = v.astype(jnp.bfloat16)
        vl = (v - vh.astype(jnp.float32)).astype(jnp.bfloat16)
        mask = hi == hi_iota
        zero = jnp.zeros((), jnp.bfloat16)
        lt = jnp.concatenate([jnp.where(mask, vh, zero), jnp.where(mask, vl, zero)], axis=0)
        o = lax.dot_general(lt, rt, (((1,), (1,)), ((), ())), preferred_element_type=jnp.float32)
        out_ref[q] = o[:hi_count] + o[hi_count:]
        return carry

    lax.fori_loop(0, IMG, body, 0, unroll=IMG)


def project(weighted, idx, bins):
    n, q_count = idx.shape
    hi_count = bins // LO
    return pl.pallas_call(
        _project_kernel,
        out_shape=jax.ShapeDtypeStruct((q_count, hi_count, LO), jnp.float32),
        in_specs=[
            pl.BlockSpec(memory_space=pltpu.VMEM),
            pl.BlockSpec(memory_space=pltpu.VMEM),
        ],
        out_specs=pl.BlockSpec(memory_space=pltpu.VMEM),
        scratch_shapes=[
            pltpu.VMEM((SHIFTS, q_count, n), jnp.float32),
            pltpu.VMEM((q_count, n), jnp.int32),
        ],
        cost_estimate=pl.CostEstimate(
            flops=2 * q_count * 2 * hi_count * LO * n,
            bytes_accessed=q_count * n * (4 * SHIFTS + 4) + q_count * bins * 4,
            transcendentals=0,
        ),
    )(weighted, idx)


def shards(images, groups, references, interp_index, shell_index):
    n_cls = lax.axis_size(CLS)
    n_vol = lax.axis_size("vol")
    n_half = lax.axis_size("half")
    part_count, pix_quarter = images.shape
    class_count = references.shape[0]
    capacity = max(2 * part_count // n_cls, 4)
    slot_count = n_cls * capacity
    owner_ids = groups[:, 0]
    matches = (owner_ids[:, None] == jnp.arange(n_cls, dtype=jnp.int32)[None, :]).astype(jnp.int32)
    order_in = jnp.sum(jnp.cumsum(matches, axis=0) * matches, axis=1) - 1
    slot_ids = owner_ids * capacity + order_in
    slot_hits = slot_ids[None, :] == jnp.arange(slot_count, dtype=jnp.int32)[:, None]
    quarter_rows = pix_quarter // IMG
    bins = VOXS // IMG
    outgoing = lax.dot_general(
        slot_hits.astype(jnp.bfloat16).reshape(n_cls, capacity, part_count),
        images.reshape(part_count, quarter_rows, IMG),
        (((2,), (0,)), ((), ())),
        preferred_element_type=jnp.float32,
    ).astype(jnp.bfloat16)
    arrived = lax.all_to_all(
        jnp.swapaxes(outgoing, 1, 2), CLS, split_axis=0, concat_axis=0, tiled=True
    )
    arrived = jnp.swapaxes(arrived, 1, 2).reshape(slot_count, quarter_rows, IMG)
    shaped_refs = references.reshape(class_count, quarter_rows, IMG)
    rolled_refs = jnp.concatenate(
        [jnp.roll(shaped_refs, -(shift_id - SHIFTS // 2), axis=2) for shift_id in range(SHIFTS)],
        axis=0,
    )
    partial_scores = lax.dot_general(
        arrived, rolled_refs, (((1, 2), (1, 2)), ((), ())), preferred_element_type=jnp.float32
    )
    partial_scores = partial_scores.reshape(slot_count, SHIFTS, class_count)
    scores = exchange_sum(partial_scores, "vol")
    squares = scores * scores
    mean_square = jnp.mean(squares, axis=(1, 2), keepdims=True)
    weights = (squares / (mean_square + EPS_W)).astype(jnp.bfloat16)
    weighted = lax.dot_general(
        weights.reshape(slot_count, SHIFTS * class_count),
        arrived,
        (((0,), (0,)), ((), ())),
        preferred_element_type=jnp.float32,
    )
    slab_part = project(
        weighted.reshape(SHIFTS, class_count * quarter_rows, IMG),
        interp_index.reshape(class_count * quarter_rows, IMG),
        bins,
    )
    piece_len = VOXS // (n_half * n_cls)
    slab_part = slab_part.reshape(n_half, n_cls, piece_len)
    own_block = reduce_scatter(slab_part, "x", "z").reshape(-1)
    half_id = lax.axis_index("half")
    other_block = partner(own_block, "half", 0)
    other_shell = partner(shell_index[0], "half", 0)
    first_block = jnp.where(half_id == 0, own_block, other_block)
    second_block = jnp.where(half_id == 0, other_block, own_block)
    shell_block = jnp.where(
        half_id == 0,
        jnp.concatenate([shell_index[0], other_shell]),
        jnp.concatenate([other_shell, shell_index[0]]),
    )
    block_hot = (shell_block[:, None] == jnp.arange(NSHELL, dtype=jnp.int32)[None, :]).astype(
        jnp.float32
    )
    stats = jnp.stack([first_block * first_block, second_block * second_block, first_block * second_block])
    shell_terms = jnp.dot(stats, block_hot, precision=lax.Precision.HIGHEST)
    shell_sums = exchange_sum(exchange_sum(shell_terms, "vol"), CLS)
    shell_fsc = shell_sums[2] / (jnp.sqrt(shell_sums[0]) * jnp.sqrt(shell_sums[1]) + EPS_F)
    mean_sq = (jnp.sum(shell_sums[0]) + jnp.sum(shell_sums[1]) + 2.0 * jnp.sum(shell_sums[2])) / (
        4.0 * n_vol * VOXS
    )
    first = lax.dynamic_index_in_dim(first_block.reshape(n_half, piece_len), half_id, keepdims=False)
    second = lax.dynamic_index_in_dim(second_block.reshape(n_half, piece_len), half_id, keepdims=False)
    shell_hot = (shell_index[0][:, None] == jnp.arange(NSHELL, dtype=jnp.int32)[None, :]).astype(
        jnp.float32
    )
    filter_vox = jnp.dot(shell_hot, shell_fsc, precision=lax.Precision.HIGHEST)
    volume = filter_vox * (0.5 * (first + second)) / jnp.sqrt(mean_sq + EPS_F)
    return (volume[None, :], shell_fsc)


def solution(mesh):
    n_cls = mesh.shape["cls"]
    fine = jax.sharding.Mesh(
        mesh.devices.reshape(mesh.shape["half"], n_cls // X_CHIPS, X_CHIPS, mesh.shape["vol"]),
        ("half", "z", "x", "vol"),
    )
    rows = ("half", "z", "x")
    placed = (
        P(rows, "vol"),
        P(rows, None),
        P(CLS, "vol"),
        P(CLS, "vol"),
        P("vol", rows),
    )
    return jax.shard_map(
        shards,
        mesh=fine,
        in_specs=placed,
        out_specs=(P("vol", rows), P()),
        check_vma=False,
    )
```
